768 devices in a mesh: sec: 48 (over z_hi, y, core), tile: 16 (over z_lo, x).
Axes of the slice: x: 4, y: 8, z: 12 (z_hi: 3, z_lo: 4; z = z_hi * 4 + z_lo), core: 2. Of those that a mesh axis runs over, the one named last changes fastest.
Arguments:
- sections: bfloat16 [96, 2048, 128], P('sec', 'tile'), may hold values from -6 to 6
- offsets: int32 [96], P('sec'), may hold values from 1 to 2
- valid_mask: int32 [96, 16], P('sec', 'tile'), may hold values 0 or 1
- conv1_w: bfloat16 [9, 16], replicated, may hold values from -2 to 2
- conv1_b: float32 [16], replicated, may hold values from -3 to 3
- conv2_w: bfloat16 [9, 16, 16], replicated, may hold values from -0.5 to 0.5
Outputs:
- residual: float32 [2, 96, 16], P(None, 'sec', 'tile')
- affine: float32 [96, 4], P('sec')
The draws below stay inside these ranges and needn't reach their ends.
All inputs are finite; a program needn't handle non-finite values. No bound on the sum of `valid_mask` on one device may be relied on, other than what follows from the above.
Results may differ from the reference program's by a relative error of at most 0.0085.
The reference program's roundings to bfloat16 on the way count: a program that leaves them out, or rounds other values in their place, can miss the bound.
Values may be sent and summed in bfloat16 or wider, within the bound.
No kernel may reach another device: no remote copies, remote signals or barrier semaphores. Data moves between devices by JAX's collectives and lax.ppermute only.
A program may use at most 32 MiB of HBM per device.

```python
import math
import jax
import jax.numpy as jnp
from jax import lax

CH = 16
P_SIZE = 128
SECTIONS = 96
NPY = 16
H = 2048


def draw_sections(key, part):
    values = jnp.clip(jax.random.normal(key, (SECTIONS, H, P_SIZE), jnp.float32), -6.0, 6.0)
    return values.astype(jnp.bfloat16)


def touch_ends(drawn, stream_key, least, largest):
    dims = drawn.shape
    spot = [jax.random.randint(jax.random.fold_in(stream_key, axis), (), 0, dims[axis]) for axis in range(len(dims))]
    drawn = drawn.at[tuple(spot)].set(least)
    longest = dims.index(max(dims))
    spot[longest] = (spot[longest] + 1) % dims[longest]
    return drawn.at[tuple(spot)].set(largest)


def gaussian(rng, dims, deviation, most, kind=jnp.bfloat16):
    values = jax.random.normal(rng, dims, jnp.float32) * deviation
    return jnp.minimum(jnp.maximum(values, -most), most).astype(kind)


def setup_inputs(seed: int = 0) -> dict:
    key_list = jax.random.split(jax.random.key(seed), 7)
    return {
        "sections": draw_sections(jax.random.fold_in(key_list[6], 71), 0),
        "offsets": touch_ends(jax.random.randint(key_list[1], (SECTIONS,), 1, 3), jax.random.fold_in(key_list[1], 1), 1, 2).astype(jnp.int32),
        "valid_mask": touch_ends((jax.random.randint(key_list[2], (SECTIONS, NPY), 0, 4) < 3).astype(jnp.int32), jax.random.fold_in(key_list[2], 1), 0, 1),
        "conv1_w": gaussian(key_list[3], (9, CH), 9 ** -0.5, 2.0),
        "conv1_b": gaussian(key_list[4], (CH,), 0.5, 3.0, jnp.float32),
        "conv2_w": gaussian(key_list[5], (9, CH, CH), (9 * CH) ** -0.5, 0.5),
    }


RIDGE_TERM = 1.0
CORR_GAIN = 2.5
FLOW_UNIT = 8.0

def dft_tables():
    index_row = jnp.arange(P_SIZE, dtype=jnp.int32)
    product = index_row[:, None] * index_row[None, :] % P_SIZE
    phase_angle = product.astype(jnp.float32) * (2.0 * math.pi / P_SIZE)
    return (jnp.cos(phase_angle).astype(jnp.bfloat16), jnp.sin(phase_angle).astype(jnp.bfloat16))

def section_features(image_rows, conv1_w, conv1_b, conv2_w):
    rows_count = image_rows.shape[0]
    padded = jnp.pad(image_rows.astype(jnp.float32), 1)
    layer_one = jnp.zeros((CH, rows_count, P_SIZE), jnp.float32) + conv1_b[:, None, None]
    for tap_row in range(3):
        for tap_col in range(3):
            weight_tap = conv1_w[3 * tap_row + tap_col].astype(jnp.float32)
            window = padded[tap_row:tap_row + rows_count, tap_col:tap_col + P_SIZE]
            layer_one = layer_one + weight_tap[:, None, None] * window[None]
    hidden = jax.nn.relu(layer_one).astype(jnp.bfloat16)
    hidden_pad = jnp.pad(hidden, ((0, 0), (1, 1), (1, 1)))
    layer_two = jnp.zeros((CH, rows_count, P_SIZE), jnp.float32)
    for tap_row in range(3):
        for tap_col in range(3):
            window = hidden_pad[:, tap_row:tap_row + rows_count, tap_col:tap_col + P_SIZE].astype(jnp.float32)
            weight_tap = conv2_w[3 * tap_row + tap_col].astype(jnp.float32)
            layer_two = layer_two + jnp.einsum('chw,co->ohw', window, weight_tap)
    return layer_two.astype(jnp.bfloat16)

def patch_spectra(patches, cosine, sin_table):
    flat_rows = patches.reshape(-1, P_SIZE)
    half_cos = jnp.dot(flat_rows, cosine, preferred_element_type=jnp.float32).astype(jnp.bfloat16)
    half_sin = jnp.dot(flat_rows, sin_table, preferred_element_type=jnp.float32).astype(jnp.bfloat16)
    half_cos = half_cos.reshape(patches.shape).astype(jnp.float32)
    half_sin = half_sin.reshape(patches.shape).astype(jnp.float32)
    cos_wide = cosine.astype(jnp.float32)
    sin_wide = sin_table.astype(jnp.float32)
    spec_real = jnp.einsum('uy,byk->buk', cos_wide, half_cos) - jnp.einsum('uy,byk->buk', sin_wide, half_sin)
    spec_imag = -(jnp.einsum('uy,byk->buk', sin_wide, half_cos) + jnp.einsum('uy,byk->buk', cos_wide, half_sin))
    return (spec_real.astype(jnp.bfloat16), spec_imag.astype(jnp.bfloat16))

def flows_of(own_real, own_imag, part_real, part_imag, cosine, sin_table):
    own_re32 = own_real.astype(jnp.float32)
    own_im32 = own_imag.astype(jnp.float32)
    part_re32 = part_real.astype(jnp.float32)
    part_im32 = part_imag.astype(jnp.float32)
    freq_index = jnp.arange(P_SIZE, dtype=jnp.int32)
    zero_freq = (freq_index[:, None] == 0) & (freq_index[None, :] == 0)
    cross_real = lax.optimization_barrier(jnp.sum(own_re32 * part_re32 + own_im32 * part_im32, axis=1)).astype(jnp.bfloat16)
    cross_imag = lax.optimization_barrier(jnp.sum(own_re32 * part_im32 - own_im32 * part_re32, axis=1)).astype(jnp.bfloat16)
    cross_real = jnp.where(zero_freq[None], jnp.zeros_like(cross_real), cross_real)
    cross_imag = jnp.where(zero_freq[None], jnp.zeros_like(cross_imag), cross_imag)
    patch_count = cross_real.shape[0]
    flat_real = cross_real.reshape(-1, P_SIZE)
    flat_imag = cross_imag.reshape(-1, P_SIZE)
    back_real = (jnp.dot(flat_real, cosine, preferred_element_type=jnp.float32) - jnp.dot(flat_imag, sin_table, preferred_element_type=jnp.float32)).astype(jnp.bfloat16)
    back_imag = (jnp.dot(flat_real, sin_table, preferred_element_type=jnp.float32) + jnp.dot(flat_imag, cosine, preferred_element_type=jnp.float32)).astype(jnp.bfloat16)
    back_real = back_real.reshape(patch_count, P_SIZE, P_SIZE).astype(jnp.float32)
    back_imag = back_imag.reshape(patch_count, P_SIZE, P_SIZE).astype(jnp.float32)
    raw_corr = jnp.einsum('ju,buk->bjk', cosine.astype(jnp.float32), back_real) - jnp.einsum('ju,buk->bjk', sin_table.astype(jnp.float32), back_imag)
    scores = raw_corr * (CORR_GAIN / (P_SIZE * P_SIZE * P_SIZE * math.sqrt(CH)))
    flat_scores = scores.reshape(patch_count, P_SIZE * P_SIZE)
    row_max = lax.optimization_barrier(jnp.max(flat_scores, axis=1, keepdims=True))
    expos = jnp.exp(flat_scores - row_max)
    probability = expos / lax.optimization_barrier(jnp.sum(expos, axis=1, keepdims=True))
    lag_index = jnp.arange(P_SIZE, dtype=jnp.int32)
    signed_lag = jnp.where(lag_index >= P_SIZE // 2, lag_index - P_SIZE, lag_index).astype(jnp.float32)
    lag_rows = jnp.broadcast_to(signed_lag[:, None], (P_SIZE, P_SIZE)).reshape(-1)
    lag_cols = jnp.broadcast_to(signed_lag[None, :], (P_SIZE, P_SIZE)).reshape(-1)
    flow_rows = lax.optimization_barrier(jnp.sum(probability * lag_rows[None], axis=1)) / FLOW_UNIT
    flow_cols = lax.optimization_barrier(jnp.sum(probability * lag_cols[None], axis=1)) / FLOW_UNIT
    return jnp.stack([flow_rows, flow_cols], axis=0)

def reference(sections, offsets, valid_mask, conv1_w, conv1_b, conv2_w):
    cosine, sin_table = dft_tables()

    def to_spectra(section_image):
        feats = section_features(section_image, conv1_w, conv1_b, conv2_w)
        patches = feats.reshape(CH, NPY, P_SIZE, P_SIZE).transpose(1, 0, 2, 3).reshape(NPY * CH, P_SIZE, P_SIZE)
        spec_real, spec_imag = patch_spectra(patches, cosine, sin_table)
        return (spec_real.reshape(NPY, CH, P_SIZE, P_SIZE), spec_imag.reshape(NPY, CH, P_SIZE, P_SIZE))

    def scan_step(carry, inputs):
        next_one, next_two = carry
        section_image, offset_value, mask_row, section_id = inputs
        own_spec = to_spectra(section_image)
        use_first = offset_value == 1
        part_real = jnp.where(use_first, next_one[0], next_two[0])
        part_imag = jnp.where(use_first, next_one[1], next_two[1])
        flow_est = flows_of(own_spec[0], own_spec[1], part_real, part_imag, cosine, sin_table)
        pair_ok = jnp.where(section_id + offset_value < SECTIONS, 1.0, 0.0).astype(jnp.float32)
        weights = mask_row.astype(jnp.float32) * pair_ok
        return ((own_spec, next_one), (flow_est, weights))
    zero_spec = jnp.zeros((NPY, CH, P_SIZE, P_SIZE), jnp.bfloat16)
    start = ((zero_spec, zero_spec), (zero_spec, zero_spec))
    section_ids = jnp.arange(SECTIONS, dtype=jnp.int32)
    _, (flow_all, weights) = lax.scan(scan_step, start, (sections, offsets, valid_mask, section_ids), reverse=True)
    flow_est = flow_all.transpose(1, 0, 2)
    grid_y = (jnp.arange(NPY, dtype=jnp.int32).astype(jnp.float32) + 0.5) / NPY * 2.0 - 1.0
    weight_sum = lax.optimization_barrier(jnp.sum(weights, axis=1))
    weighted_y = lax.optimization_barrier(jnp.sum(weights * grid_y[None], axis=1))
    weighted_yy = lax.optimization_barrier(jnp.sum(weights * grid_y[None] * grid_y[None], axis=1))
    flow_sum = lax.optimization_barrier(jnp.sum(flow_est * weights[None], axis=2))
    flow_y_sum = lax.optimization_barrier(jnp.sum(flow_est * (weights * grid_y[None])[None], axis=2))
    m_zero = weight_sum + RIDGE_TERM
    m_two = weighted_yy + RIDGE_TERM
    determinant = m_zero * m_two - weighted_y * weighted_y
    offset_coef = (m_two[None] * flow_sum - weighted_y[None] * flow_y_sum) / determinant[None]
    slope_coef = (m_zero[None] * flow_y_sum - weighted_y[None] * flow_sum) / determinant[None]
    affine = jnp.stack([offset_coef[0], slope_coef[0], offset_coef[1], slope_coef[1]], axis=1)
    fitted = offset_coef[:, :, None] + slope_coef[:, :, None] * grid_y[None, None, :]
    residual = (flow_est - fitted) * weights[None]
    return (residual, affine)
```

```python
import math

import jax
import jax.numpy as jnp
from jax import lax
from jax.sharding import PartitionSpec as P

RIDGE_TERM = 1.0
CORR_GAIN = 2.5
FLOW_UNIT = 8.0


def with_halo(x, sides, width):
    for axis, dim in sides:
        peers, length = (lax.axis_size(axis), x.shape[dim])
        up = [(i, (i + 1) % peers) for i in range(peers - 1)]
        down = [(j, i) for i, j in up]
        last = lax.slice_in_dim(x, length - width, length, axis=dim)
        initial = lax.slice_in_dim(x, 0, width, axis=dim)
        before = lax.ppermute(last, axis, up)
        after = lax.ppermute(initial, axis, down)
        x = jnp.concatenate([before, x, after], axis=dim)
    return x


def from_behind(block, axis, distance):
    devices = range(lax.axis_size(axis))
    route = [(i - distance, i) for i in devices if i - distance in devices]
    return lax.ppermute(block, axis, route)


def tile_sum(v, axis):
    peers = lax.axis_size(axis)
    if peers & (peers - 1):
        return lax.psum(v, axis)
    step = 1
    while step < peers:
        v = v + lax.ppermute(v, axis, [(i, i ^ step) for i in range(peers)])
        step *= 2
    return v


def dft_tables(patch_len):
    index_row = jnp.arange(patch_len, dtype=jnp.int32)
    product = index_row[:, None] * index_row[None, :] % patch_len
    phase_angle = product.astype(jnp.float32) * (2.0 * math.pi / patch_len)
    return (jnp.cos(phase_angle).astype(jnp.bfloat16), jnp.sin(phase_angle).astype(jnp.bfloat16))


def conv_layers(rows_in, inside, conv1_w, conv1_b, conv2_w):
    sec_count = rows_in.shape[0]
    wide_rows = rows_in.shape[1] - 2
    strip_rows = wide_rows - 2
    patch_len = rows_in.shape[2]
    channels = conv1_w.shape[1]
    padded = jnp.pad(rows_in, ((0, 0), (0, 0), (1, 1)))
    layer_one = (
        jnp.zeros((sec_count, channels, wide_rows, patch_len), jnp.float32)
        + conv1_b[None, :, None, None]
    )
    for tap_row in range(3):
        for tap_col in range(3):
            weight_tap = conv1_w[3 * tap_row + tap_col].astype(jnp.float32)
            window = padded[:, tap_row : tap_row + wide_rows, tap_col : tap_col + patch_len].astype(
                jnp.float32
            )
            layer_one = layer_one + weight_tap[None, :, None, None] * window[:, None]
    hidden = jnp.where(inside[None, None, :, None], jax.nn.relu(layer_one), 0.0).astype(
        jnp.bfloat16
    )
    hidden_pad = jnp.pad(hidden, ((0, 0), (0, 0), (0, 0), (1, 1)))
    layer_two = jnp.zeros((sec_count, channels, strip_rows, patch_len), jnp.float32)
    for tap_row in range(3):
        for tap_col in range(3):
            window = hidden_pad[:, :, tap_row : tap_row + strip_rows, tap_col : tap_col + patch_len]
            layer_two = layer_two + jnp.einsum(
                "schw,co->sohw",
                window,
                conv2_w[3 * tap_row + tap_col],
                preferred_element_type=jnp.float32,
            )
    return layer_two.astype(jnp.bfloat16)


def patch_spectra(features, cosine, sin_table, rows_per):
    sec_count, channels, strip_rows, patch_len = features.shape
    patches = features.reshape(sec_count, channels, rows_per, patch_len, patch_len)
    patches = patches.transpose(0, 2, 1, 3, 4).reshape(-1, patch_len, patch_len)
    flat_rows = patches.reshape(-1, patch_len)
    half_cos = (
        jnp.dot(flat_rows, cosine, preferred_element_type=jnp.float32)
        .astype(jnp.bfloat16)
        .reshape(patches.shape)
    )
    half_sin = (
        jnp.dot(flat_rows, sin_table, preferred_element_type=jnp.float32)
        .astype(jnp.bfloat16)
        .reshape(patches.shape)
    )
    spec_real = jnp.einsum(
        "uy,byk->buk", cosine, half_cos, preferred_element_type=jnp.float32
    ) - jnp.einsum("uy,byk->buk", sin_table, half_sin, preferred_element_type=jnp.float32)
    spec_imag = -(
        jnp.einsum("uy,byk->buk", sin_table, half_cos, preferred_element_type=jnp.float32)
        + jnp.einsum("uy,byk->buk", cosine, half_sin, preferred_element_type=jnp.float32)
    )
    out_shape = (sec_count, rows_per, channels, patch_len, patch_len)
    return (
        spec_real.astype(jnp.bfloat16).reshape(out_shape),
        spec_imag.astype(jnp.bfloat16).reshape(out_shape),
    )


def correlate(own_real, own_imag, part_real, part_imag, cosine, sin_table):
    patch_len = own_real.shape[-1]
    channels = own_real.shape[2]
    own_re32 = own_real.astype(jnp.float32)
    own_im32 = own_imag.astype(jnp.float32)
    part_re32 = part_real.astype(jnp.float32)
    part_im32 = part_imag.astype(jnp.float32)
    freq_index = jnp.arange(patch_len, dtype=jnp.int32)
    zero_freq = (freq_index[:, None] == 0) & (freq_index[None, :] == 0)
    cross_real = jnp.sum(own_re32 * part_re32 + own_im32 * part_im32, axis=2).astype(jnp.bfloat16)
    cross_imag = jnp.sum(own_re32 * part_im32 - own_im32 * part_re32, axis=2).astype(jnp.bfloat16)
    cross_real = jnp.where(zero_freq[None, None], jnp.zeros_like(cross_real), cross_real)
    cross_imag = jnp.where(zero_freq[None, None], jnp.zeros_like(cross_imag), cross_imag)
    flat_real = cross_real.reshape(-1, patch_len)
    flat_imag = cross_imag.reshape(-1, patch_len)
    back_real = (
        jnp.dot(flat_real, cosine, preferred_element_type=jnp.float32)
        - jnp.dot(flat_imag, sin_table, preferred_element_type=jnp.float32)
    ).astype(jnp.bfloat16)
    back_imag = (
        jnp.dot(flat_real, sin_table, preferred_element_type=jnp.float32)
        + jnp.dot(flat_imag, cosine, preferred_element_type=jnp.float32)
    ).astype(jnp.bfloat16)
    back_real = back_real.reshape(-1, patch_len, patch_len)
    back_imag = back_imag.reshape(-1, patch_len, patch_len)
    raw_corr = jnp.einsum(
        "ju,buk->bjk", cosine, back_real, preferred_element_type=jnp.float32
    ) - jnp.einsum("ju,buk->bjk", sin_table, back_imag, preferred_element_type=jnp.float32)
    scores = raw_corr * (CORR_GAIN / (patch_len * patch_len * patch_len * math.sqrt(channels)))
    flat_scores = scores.reshape(-1, patch_len * patch_len)
    row_max = jnp.max(flat_scores, axis=1, keepdims=True)
    expos = jnp.exp(flat_scores - row_max)
    probability = expos / jnp.sum(expos, axis=1, keepdims=True)
    lag_index = jnp.arange(patch_len, dtype=jnp.int32)
    signed_lag = jnp.where(lag_index >= patch_len // 2, lag_index - patch_len, lag_index).astype(
        jnp.float32
    )
    lag_rows = jnp.broadcast_to(signed_lag[:, None], (patch_len, patch_len)).reshape(-1)
    lag_cols = jnp.broadcast_to(signed_lag[None, :], (patch_len, patch_len)).reshape(-1)
    flow_rows = jnp.sum(probability * lag_rows[None], axis=1) / FLOW_UNIT
    flow_cols = jnp.sum(probability * lag_cols[None], axis=1) / FLOW_UNIT
    return jnp.stack([flow_rows, flow_cols], axis=0)


def local(sections, offsets, valid_mask, conv1_w, conv1_b, conv2_w):
    sec_here = sections.shape[0]
    strip_rows = sections.shape[1]
    patch_len = sections.shape[2]
    rows_per = strip_rows // patch_len
    tile_count = lax.axis_size("tile")
    tile_pos = lax.axis_index("tile")
    cosine, sin_table = dft_tables(patch_len)
    padded_rows = with_halo(sections, (("tile", 1),), 2)
    row_global = tile_pos * strip_rows - 1 + jnp.arange(strip_rows + 2, dtype=jnp.int32)
    inside = (row_global >= 0) & (row_global < strip_rows * tile_count)
    own_feats = conv_layers(padded_rows, inside, conv1_w, conv1_b, conv2_w)
    own_real, own_imag = patch_spectra(own_feats, cosine, sin_table, rows_per)
    next_feats = from_behind(own_feats, "sec", -1)
    next_real, next_imag = patch_spectra(next_feats, cosine, sin_table, rows_per)
    combined_real = jnp.concatenate([own_real, next_real], axis=0)
    combined_imag = jnp.concatenate([own_imag, next_imag], axis=0)
    use_first = (offsets == 1)[:, None, None, None, None]
    part_real = jnp.where(
        use_first, combined_real[1 : sec_here + 1], combined_real[2 : sec_here + 2]
    )
    part_imag = jnp.where(
        use_first, combined_imag[1 : sec_here + 1], combined_imag[2 : sec_here + 2]
    )
    flow_est = correlate(own_real, own_imag, part_real, part_imag, cosine, sin_table).reshape(
        2, sec_here, rows_per
    )
    section_ids = lax.axis_index("sec") * sec_here + jnp.arange(sec_here, dtype=jnp.int32)
    total_sections = sec_here * lax.axis_size("sec")
    pair_ok = jnp.where(section_ids + offsets < total_sections, 1.0, 0.0).astype(jnp.float32)
    weights = valid_mask.astype(jnp.float32) * pair_ok[:, None]
    rows_all = rows_per * tile_count
    grid_y = (
        (tile_pos * rows_per + jnp.arange(rows_per, dtype=jnp.int32)).astype(jnp.float32) + 0.5
    ) / rows_all * 2.0 - 1.0
    weight_y = weights * grid_y[None]
    partial = jnp.concatenate(
        [
            jnp.sum(weights, axis=1)[:, None],
            jnp.sum(weight_y, axis=1)[:, None],
            jnp.sum(weight_y * grid_y[None], axis=1)[:, None],
            jnp.sum(flow_est * weights[None], axis=2).T,
            jnp.sum(flow_est * weight_y[None], axis=2).T,
        ],
        axis=1,
    )
    totals = tile_sum(partial, "tile")
    weight_sum, weighted_y, weighted_yy = totals[:, 0], totals[:, 1], totals[:, 2]
    flow_sum = totals[:, 3:5].T
    flow_y_sum = totals[:, 5:7].T
    m_zero = weight_sum + RIDGE_TERM
    m_two = weighted_yy + RIDGE_TERM
    determinant = m_zero * m_two - weighted_y * weighted_y
    offset_coef = (m_two[None] * flow_sum - weighted_y[None] * flow_y_sum) / determinant[None]
    slope_coef = (m_zero[None] * flow_y_sum - weighted_y[None] * flow_sum) / determinant[None]
    affine = jnp.stack([offset_coef[0], slope_coef[0], offset_coef[1], slope_coef[1]], axis=1)
    fitted = offset_coef[:, :, None] + slope_coef[:, :, None] * grid_y[None, None, :]
    residual = (flow_est - fitted) * weights[None]
    return (residual, affine)


def solution(mesh):
    placed = (P("sec", "tile", None), P("sec"), P("sec", "tile"), P(), P(), P())
    return jax.shard_map(
        local,
        mesh=mesh,
        in_specs=placed,
        out_specs=(P(None, "sec", "tile"), P("sec", None)),
        check_vma=False,
    )
```

```python
import math

import jax
import jax.numpy as jnp
from jax import lax
from jax.sharding import PartitionSpec as P

RIDGE_TERM = 1.0
CORR_GAIN = 2.5
FLOW_UNIT = 8.0


def with_halo(x, sides, width):
    for axis, dim in sides:
        peers, length = (lax.axis_size(axis), x.shape[dim])
        up = [(i, (i + 1) % peers) for i in range(peers - 1)]
        down = [(j, i) for i, j in up]
        last = lax.slice_in_dim(x, length - width, length, axis=dim)
        initial = lax.slice_in_dim(x, 0, width, axis=dim)
        before = lax.ppermute(last, axis, up)
        after = lax.ppermute(initial, axis, down)
        x = jnp.concatenate([before, x, after], axis=dim)
    return x


def from_behind(block, axis, distance):
    devices = range(lax.axis_size(axis))
    route = [(i - distance, i) for i in devices if i - distance in devices]
    return lax.ppermute(block, axis, route)


def tile_sum(v, axis):
    peers = lax.axis_size(axis)
    if peers & (peers - 1):
        return lax.psum(v, axis)
    step = 1
    while step < peers:
        v = v + lax.ppermute(v, axis, [(i, i ^ step) for i in range(peers)])
        step *= 2
    return v


def dft_tables(patch_len):
    index_row = jnp.arange(patch_len, dtype=jnp.int32)
    product = index_row[:, None] * index_row[None, :] % patch_len
    phase_angle = product.astype(jnp.float32) * (2.0 * math.pi / patch_len)
    return (jnp.cos(phase_angle).astype(jnp.bfloat16), jnp.sin(phase_angle).astype(jnp.bfloat16))


def conv_layers(rows_in, inside, conv1_w, conv1_b, conv2_w):
    sec_count = rows_in.shape[0]
    wide_rows = rows_in.shape[1] - 2
    strip_rows = wide_rows - 2
    patch_len = rows_in.shape[2]
    channels = conv1_w.shape[1]
    padded = jnp.pad(rows_in, ((0, 0), (0, 0), (1, 1)))
    layer_one = (
        jnp.zeros((sec_count, channels, wide_rows, patch_len), jnp.float32)
        + conv1_b[None, :, None, None]
    )
    for tap_row in range(3):
        for tap_col in range(3):
            weight_tap = conv1_w[3 * tap_row + tap_col].astype(jnp.float32)
            window = padded[:, tap_row : tap_row + wide_rows, tap_col : tap_col + patch_len].astype(
                jnp.float32
            )
            layer_one = layer_one + weight_tap[None, :, None, None] * window[:, None]
    hidden = jnp.where(inside[None, None, :, None], jax.nn.relu(layer_one), 0.0).astype(
        jnp.bfloat16
    )
    hidden_pad = jnp.pad(hidden, ((0, 0), (0, 0), (0, 0), (1, 1)))
    layer_two = jnp.zeros((sec_count, channels, strip_rows, patch_len), jnp.float32)
    for tap_row in range(3):
        for tap_col in range(3):
            window = hidden_pad[:, :, tap_row : tap_row + strip_rows, tap_col : tap_col + patch_len]
            layer_two = layer_two + jnp.einsum(
                "schw,co->sohw",
                window,
                conv2_w[3 * tap_row + tap_col],
                preferred_element_type=jnp.float32,
            )
    return layer_two.astype(jnp.bfloat16)


def patch_spectra(features, cosine, sin_table, rows_per):
    sec_count, channels, strip_rows, patch_len = features.shape
    patches = features.reshape(sec_count, channels, rows_per, patch_len, patch_len)
    patches = patches.transpose(0, 2, 1, 3, 4).reshape(-1, patch_len, patch_len)
    flat_rows = patches.reshape(-1, patch_len)
    half_cos = (
        jnp.dot(flat_rows, cosine, preferred_element_type=jnp.float32)
        .astype(jnp.bfloat16)
        .reshape(patches.shape)
    )
    half_sin = (
        jnp.dot(flat_rows, sin_table, preferred_element_type=jnp.float32)
        .astype(jnp.bfloat16)
        .reshape(patches.shape)
    )
    spec_real = jnp.einsum(
        "uy,byk->buk", cosine, half_cos, preferred_element_type=jnp.float32
    ) - jnp.einsum("uy,byk->buk", sin_table, half_sin, preferred_element_type=jnp.float32)
    spec_imag = -(
        jnp.einsum("uy,byk->buk", sin_table, half_cos, preferred_element_type=jnp.float32)
        + jnp.einsum("uy,byk->buk", cosine, half_sin, preferred_element_type=jnp.float32)
    )
    out_shape = (sec_count, rows_per, channels, patch_len, patch_len)
    return (
        spec_real.astype(jnp.bfloat16).reshape(out_shape),
        spec_imag.astype(jnp.bfloat16).reshape(out_shape),
    )


def correlate(own_real, own_imag, part_real, part_imag, pair_valid, cosine, sin_table):
    patch_len = own_real.shape[-1]
    channels = own_real.shape[2]
    own_re32 = own_real.astype(jnp.float32)
    own_im32 = own_imag.astype(jnp.float32)
    part_re32 = part_real.astype(jnp.float32)
    part_im32 = part_imag.astype(jnp.float32)
    freq_index = jnp.arange(patch_len, dtype=jnp.int32)
    zero_freq = (freq_index[:, None] == 0) & (freq_index[None, :] == 0)
    cross_real = jnp.sum(own_re32 * part_re32 + own_im32 * part_im32, axis=2).astype(jnp.bfloat16)
    cross_imag = jnp.sum(own_re32 * part_im32 - own_im32 * part_re32, axis=2).astype(jnp.bfloat16)
    drop = zero_freq[None, None] | ~pair_valid[:, None, None, None]
    cross_real = jnp.where(drop, jnp.zeros_like(cross_real), cross_real)
    cross_imag = jnp.where(drop, jnp.zeros_like(cross_imag), cross_imag)
    flat_real = cross_real.reshape(-1, patch_len)
    flat_imag = cross_imag.reshape(-1, patch_len)
    back_real = (
        jnp.dot(flat_real, cosine, preferred_element_type=jnp.float32)
        - jnp.dot(flat_imag, sin_table, preferred_element_type=jnp.float32)
    ).astype(jnp.bfloat16)
    back_imag = (
        jnp.dot(flat_real, sin_table, preferred_element_type=jnp.float32)
        + jnp.dot(flat_imag, cosine, preferred_element_type=jnp.float32)
    ).astype(jnp.bfloat16)
    back_real = back_real.reshape(-1, patch_len, patch_len)
    back_imag = back_imag.reshape(-1, patch_len, patch_len)
    raw_corr = jnp.einsum(
        "ju,buk->bjk", cosine, back_real, preferred_element_type=jnp.float32
    ) - jnp.einsum("ju,buk->bjk", sin_table, back_imag, preferred_element_type=jnp.float32)
    scores = raw_corr * (CORR_GAIN / (patch_len * patch_len * patch_len * math.sqrt(channels)))
    flat_scores = scores.reshape(-1, patch_len * patch_len)
    row_max = jnp.max(flat_scores, axis=1, keepdims=True)
    expos = jnp.exp(flat_scores - row_max)
    probability = expos / jnp.sum(expos, axis=1, keepdims=True)
    lag_index = jnp.arange(patch_len, dtype=jnp.int32)
    signed_lag = jnp.where(lag_index >= patch_len // 2, lag_index - patch_len, lag_index).astype(
        jnp.float32
    )
    lag_rows = jnp.broadcast_to(signed_lag[:, None], (patch_len, patch_len)).reshape(-1)
    lag_cols = jnp.broadcast_to(signed_lag[None, :], (patch_len, patch_len)).reshape(-1)
    flow_rows = jnp.sum(probability * lag_rows[None], axis=1) / FLOW_UNIT
    flow_cols = jnp.sum(probability * lag_cols[None], axis=1) / FLOW_UNIT
    return jnp.stack([flow_rows, flow_cols], axis=0)


def local(sections, offsets, valid_mask, conv1_w, conv1_b, conv2_w):
    sec_here = sections.shape[0]
    strip_rows = sections.shape[1]
    patch_len = sections.shape[2]
    rows_per = strip_rows // patch_len
    tile_count = lax.axis_size("tile")
    tile_pos = lax.axis_index("tile")
    cosine, sin_table = dft_tables(patch_len)
    padded_rows = with_halo(sections, (("tile", 1),), 2)
    next_rows = from_behind(padded_rows, "sec", -1)
    row_global = tile_pos * strip_rows - 1 + jnp.arange(strip_rows + 2, dtype=jnp.int32)
    inside = (row_global >= 0) & (row_global < strip_rows * tile_count)
    all_rows = jnp.concatenate([padded_rows, next_rows], axis=0)
    all_feats = conv_layers(all_rows, inside, conv1_w, conv1_b, conv2_w)
    combined_real, combined_imag = patch_spectra(all_feats, cosine, sin_table, rows_per)
    own_real, own_imag = combined_real[:sec_here], combined_imag[:sec_here]
    use_first = (offsets == 1)[:, None, None, None, None]
    part_real = jnp.where(
        use_first, combined_real[1 : sec_here + 1], combined_real[2 : sec_here + 2]
    )
    part_imag = jnp.where(
        use_first, combined_imag[1 : sec_here + 1], combined_imag[2 : sec_here + 2]
    )
    section_ids = lax.axis_index("sec") * sec_here + jnp.arange(sec_here, dtype=jnp.int32)
    total_sections = sec_here * lax.axis_size("sec")
    pair_valid = section_ids + offsets < total_sections
    flow_est = correlate(
        own_real, own_imag, part_real, part_imag, pair_valid, cosine, sin_table
    ).reshape(2, sec_here, rows_per)
    pair_ok = jnp.where(pair_valid, 1.0, 0.0).astype(jnp.float32)
    weights = valid_mask.astype(jnp.float32) * pair_ok[:, None]
    rows_all = rows_per * tile_count
    grid_y = (
        (tile_pos * rows_per + jnp.arange(rows_per, dtype=jnp.int32)).astype(jnp.float32) + 0.5
    ) / rows_all * 2.0 - 1.0
    weight_y = weights * grid_y[None]
    partial = jnp.concatenate(
        [
            jnp.sum(weights, axis=1)[:, None],
            jnp.sum(weight_y, axis=1)[:, None],
            jnp.sum(weight_y * grid_y[None], axis=1)[:, None],
            jnp.sum(flow_est * weights[None], axis=2).T,
            jnp.sum(flow_est * weight_y[None], axis=2).T,
        ],
        axis=1,
    )
    totals = tile_sum(partial, "tile")
    weight_sum, weighted_y, weighted_yy = totals[:, 0], totals[:, 1], totals[:, 2]
    flow_sum = totals[:, 3:5].T
    flow_y_sum = totals[:, 5:7].T
    m_zero = weight_sum + RIDGE_TERM
    m_two = weighted_yy + RIDGE_TERM
    determinant = m_zero * m_two - weighted_y * weighted_y
    offset_coef = (m_two[None] * flow_sum - weighted_y[None] * flow_y_sum) / determinant[None]
    slope_coef = (m_zero[None] * flow_y_sum - weighted_y[None] * flow_sum) / determinant[None]
    affine = jnp.stack([offset_coef[0], slope_coef[0], offset_coef[1], slope_coef[1]], axis=1)
    fitted = offset_coef[:, :, None] + slope_coef[:, :, None] * grid_y[None, None, :]
    residual = (flow_est - fitted) * weights[None]
    return (residual, affine)


def solution(mesh):
    placed = (P("sec", "tile", None), P("sec"), P("sec", "tile"), P(), P(), P())
    return jax.shard_map(
        local,
        mesh=mesh,
        in_specs=placed,
        out_specs=(P(None, "sec", "tile"), P("sec", None)),
        check_vma=False,
    )
```

```python
import math

import jax
import jax.numpy as jnp
from jax import lax
from jax.sharding import PartitionSpec as P

RIDGE_TERM = 1.0
CORR_GAIN = 2.5
FLOW_UNIT = 8.0


def with_halo(x, sides, width):
    for axis, dim in sides:
        peers, length = (lax.axis_size(axis), x.shape[dim])
        up = [(i, (i + 1) % peers) for i in range(peers - 1)]
        down = [(j, i) for i, j in up]
        last = lax.slice_in_dim(x, length - width, length, axis=dim)
        initial = lax.slice_in_dim(x, 0, width, axis=dim)
        before = lax.ppermute(last, axis, up)
        after = lax.ppermute(initial, axis, down)
        x = jnp.concatenate([before, x, after], axis=dim)
    return x


def from_behind(block, axis, distance):
    devices = range(lax.axis_size(axis))
    route = [(i - distance, i) for i in devices if i - distance in devices]
    return lax.ppermute(block, axis, route)


def tile_sum(v, axis):
    peers = lax.axis_size(axis)
    if peers & (peers - 1):
        return lax.psum(v, axis)
    step = 1
    while step < peers:
        v = v + lax.ppermute(v, axis, [(i, i ^ step) for i in range(peers)])
        step *= 2
    return v


def dft_tables(patch_len):
    index_row = jnp.arange(patch_len, dtype=jnp.int32)
    product = index_row[:, None] * index_row[None, :] % patch_len
    phase_angle = product.astype(jnp.float32) * (2.0 * math.pi / patch_len)
    return (jnp.cos(phase_angle).astype(jnp.bfloat16), jnp.sin(phase_angle).astype(jnp.bfloat16))


def conv_layers(rows_in, inside, conv1_w, conv1_b, conv2_w):
    sec_count = rows_in.shape[0]
    wide_rows = rows_in.shape[1] - 2
    strip_rows = wide_rows - 2
    patch_len = rows_in.shape[2]
    channels = conv1_w.shape[1]
    padded = jnp.pad(rows_in, ((0, 0), (0, 0), (1, 1)))
    layer_one = (
        jnp.zeros((sec_count, channels, wide_rows, patch_len), jnp.float32)
        + conv1_b[None, :, None, None]
    )
    for tap_row in range(3):
        for tap_col in range(3):
            weight_tap = conv1_w[3 * tap_row + tap_col].astype(jnp.float32)
            window = padded[:, tap_row : tap_row + wide_rows, tap_col : tap_col + patch_len].astype(
                jnp.float32
            )
            layer_one = layer_one + weight_tap[None, :, None, None] * window[:, None]
    hidden = jnp.where(inside[None, None, :, None], jax.nn.relu(layer_one), 0.0).astype(
        jnp.bfloat16
    )
    hidden_pad = jnp.pad(hidden, ((0, 0), (0, 0), (0, 0), (1, 1)))
    layer_two = jnp.zeros((sec_count, channels, strip_rows, patch_len), jnp.float32)
    for tap_row in range(3):
        for tap_col in range(3):
            window = hidden_pad[:, :, tap_row : tap_row + strip_rows, tap_col : tap_col + patch_len]
            layer_two = layer_two + jnp.einsum(
                "schw,co->sohw",
                window,
                conv2_w[3 * tap_row + tap_col],
                preferred_element_type=jnp.float32,
            )
    return layer_two.astype(jnp.bfloat16)


def patch_spectra(features, cosine, sin_table, rows_per):
    sec_count, channels, strip_rows, patch_len = features.shape
    patches = features.reshape(sec_count, channels, rows_per, patch_len, patch_len)
    patches = patches.transpose(0, 2, 1, 3, 4).reshape(-1, patch_len, patch_len)
    flat_rows = patches.reshape(-1, patch_len)
    half_cos = (
        jnp.dot(flat_rows, cosine, preferred_element_type=jnp.float32)
        .astype(jnp.bfloat16)
        .reshape(patches.shape)
    )
    half_sin = (
        jnp.dot(flat_rows, sin_table, preferred_element_type=jnp.float32)
        .astype(jnp.bfloat16)
        .reshape(patches.shape)
    )
    spec_real = jnp.einsum(
        "uy,byk->buk", cosine, half_cos, preferred_element_type=jnp.float32
    ) - jnp.einsum("uy,byk->buk", sin_table, half_sin, preferred_element_type=jnp.float32)
    spec_imag = -(
        jnp.einsum("uy,byk->buk", sin_table, half_cos, preferred_element_type=jnp.float32)
        + jnp.einsum("uy,byk->buk", cosine, half_sin, preferred_element_type=jnp.float32)
    )
    out_shape = (sec_count, rows_per, channels, patch_len, patch_len)
    return (
        spec_real.astype(jnp.bfloat16).reshape(out_shape),
        spec_imag.astype(jnp.bfloat16).reshape(out_shape),
    )


def correlate(own_real, own_imag, part_real, part_imag, pair_valid, cosine, sin_table):
    patch_len = own_real.shape[-1]
    channels = own_real.shape[2]
    own_re32 = own_real.astype(jnp.float32)
    own_im32 = own_imag.astype(jnp.float32)
    part_re32 = part_real.astype(jnp.float32)
    part_im32 = part_imag.astype(jnp.float32)
    freq_index = jnp.arange(patch_len, dtype=jnp.int32)
    zero_freq = (freq_index[:, None] == 0) & (freq_index[None, :] == 0)
    cross_real = jnp.sum(own_re32 * part_re32 + own_im32 * part_im32, axis=2).astype(jnp.bfloat16)
    cross_imag = jnp.sum(own_re32 * part_im32 - own_im32 * part_re32, axis=2).astype(jnp.bfloat16)
    drop = zero_freq[None, None] | ~pair_valid[:, None, None, None]
    cross_real = jnp.where(drop, jnp.zeros_like(cross_real), cross_real)
    cross_imag = jnp.where(drop, jnp.zeros_like(cross_imag), cross_imag)
    flat_real = cross_real.reshape(-1, patch_len)
    flat_imag = cross_imag.reshape(-1, patch_len)
    back_real = (
        jnp.dot(flat_real, cosine, preferred_element_type=jnp.float32)
        - jnp.dot(flat_imag, sin_table, preferred_element_type=jnp.float32)
    ).astype(jnp.bfloat16)
    back_imag = (
        jnp.dot(flat_real, sin_table, preferred_element_type=jnp.float32)
        + jnp.dot(flat_imag, cosine, preferred_element_type=jnp.float32)
    ).astype(jnp.bfloat16)
    back_real = back_real.reshape(-1, patch_len, patch_len)
    back_imag = back_imag.reshape(-1, patch_len, patch_len)
    raw_corr = jnp.einsum(
        "ju,buk->bjk", cosine, back_real, preferred_element_type=jnp.float32
    ) - jnp.einsum("ju,buk->bjk", sin_table, back_imag, preferred_element_type=jnp.float32)
    scores = raw_corr * (CORR_GAIN / (patch_len * patch_len * patch_len * math.sqrt(channels)))
    flat_scores = scores.reshape(-1, patch_len * patch_len)
    row_max = jnp.max(flat_scores, axis=1, keepdims=True)
    expos = jnp.exp(flat_scores - row_max)
    probability = expos / jnp.sum(expos, axis=1, keepdims=True)
    lag_index = jnp.arange(patch_len, dtype=jnp.int32)
    signed_lag = jnp.where(lag_index >= patch_len // 2, lag_index - patch_len, lag_index).astype(
        jnp.float32
    )
    lag_rows = jnp.broadcast_to(signed_lag[:, None], (patch_len, patch_len)).reshape(-1)
    lag_cols = jnp.broadcast_to(signed_lag[None, :], (patch_len, patch_len)).reshape(-1)
    flow_rows = jnp.sum(probability * lag_rows[None], axis=1) / FLOW_UNIT
    flow_cols = jnp.sum(probability * lag_cols[None], axis=1) / FLOW_UNIT
    return jnp.stack([flow_rows, flow_cols], axis=0)


def local(sections, offsets, valid_mask, conv1_w, conv1_b, conv2_w):
    sec_here = sections.shape[0]
    strip_rows = sections.shape[1]
    patch_len = sections.shape[2]
    rows_per = strip_rows // patch_len
    tile_count = lax.axis_size("tile")
    tile_pos = lax.axis_index("tile")
    cosine, sin_table = dft_tables(patch_len)
    padded_rows = with_halo(sections, (("tile", 1),), 2)
    next_rows = from_behind(padded_rows, "sec", -1)
    row_global = tile_pos * strip_rows - 1 + jnp.arange(strip_rows + 2, dtype=jnp.int32)
    inside = (row_global >= 0) & (row_global < strip_rows * tile_count)
    own_feats = conv_layers(padded_rows, inside, conv1_w, conv1_b, conv2_w)
    own_real, own_imag = patch_spectra(own_feats, cosine, sin_table, rows_per)
    next_feats = conv_layers(next_rows, inside, conv1_w, conv1_b, conv2_w)
    next_real, next_imag = patch_spectra(next_feats, cosine, sin_table, rows_per)
    combined_real = jnp.concatenate([own_real, next_real], axis=0)
    combined_imag = jnp.concatenate([own_imag, next_imag], axis=0)
    use_first = (offsets == 1)[:, None, None, None, None]
    part_real = jnp.where(
        use_first, combined_real[1 : sec_here + 1], combined_real[2 : sec_here + 2]
    )
    part_imag = jnp.where(
        use_first, combined_imag[1 : sec_here + 1], combined_imag[2 : sec_here + 2]
    )
    section_ids = lax.axis_index("sec") * sec_here + jnp.arange(sec_here, dtype=jnp.int32)
    total_sections = sec_here * lax.axis_size("sec")
    pair_valid = section_ids + offsets < total_sections
    flow_est = correlate(
        own_real, own_imag, part_real, part_imag, pair_valid, cosine, sin_table
    ).reshape(2, sec_here, rows_per)
    pair_ok = jnp.where(pair_valid, 1.0, 0.0).astype(jnp.float32)
    weights = valid_mask.astype(jnp.float32) * pair_ok[:, None]
    rows_all = rows_per * tile_count
    grid_y = (
        (tile_pos * rows_per + jnp.arange(rows_per, dtype=jnp.int32)).astype(jnp.float32) + 0.5
    ) / rows_all * 2.0 - 1.0
    weight_y = weights * grid_y[None]
    partial = jnp.concatenate(
        [
            jnp.sum(weights, axis=1)[:, None],
            jnp.sum(weight_y, axis=1)[:, None],
            jnp.sum(weight_y * grid_y[None], axis=1)[:, None],
            jnp.sum(flow_est * weights[None], axis=2).T,
            jnp.sum(flow_est * weight_y[None], axis=2).T,
        ],
        axis=1,
    )
    totals = tile_sum(partial, "tile")
    weight_sum, weighted_y, weighted_yy = totals[:, 0], totals[:, 1], totals[:, 2]
    flow_sum = totals[:, 3:5].T
    flow_y_sum = totals[:, 5:7].T
    m_zero = weight_sum + RIDGE_TERM
    m_two = weighted_yy + RIDGE_TERM
    determinant = m_zero * m_two - weighted_y * weighted_y
    offset_coef = (m_two[None] * flow_sum - weighted_y[None] * flow_y_sum) / determinant[None]
    slope_coef = (m_zero[None] * flow_y_sum - weighted_y[None] * flow_sum) / determinant[None]
    affine = jnp.stack([offset_coef[0], slope_coef[0], offset_coef[1], slope_coef[1]], axis=1)
    fitted = offset_coef[:, :, None] + slope_coef[:, :, None] * grid_y[None, None, :]
    residual = (flow_est - fitted) * weights[None]
    return (residual, affine)


def solution(mesh):
    placed = (P("sec", "tile", None), P("sec"), P("sec", "tile"), P(), P(), P())
    return jax.shard_map(
        local,
        mesh=mesh,
        in_specs=placed,
        out_specs=(P(None, "sec", "tile"), P("sec", None)),
        check_vma=False,
    )
```

```python
import math

import jax
import jax.numpy as jnp
from jax import lax
from jax.sharding import PartitionSpec as P

RIDGE_TERM = 1.0
CORR_GAIN = 2.5
FLOW_UNIT = 8.0


def with_halo(x, sides, width):
    for axis, dim in sides:
        peers, length = (lax.axis_size(axis), x.shape[dim])
        up = [(i, (i + 1) % peers) for i in range(peers - 1)]
        down = [(j, i) for i, j in up]
        last = lax.slice_in_dim(x, length - width, length, axis=dim)
        initial = lax.slice_in_dim(x, 0, width, axis=dim)
        before = lax.ppermute(last, axis, up)
        after = lax.ppermute(initial, axis, down)
        x = jnp.concatenate([before, x, after], axis=dim)
    return x


def from_behind(block, axis, distance):
    devices = range(lax.axis_size(axis))
    route = [(i - distance, i) for i in devices if i - distance in devices]
    return lax.ppermute(block, axis, route)


def tile_sum(v, axis):
    peers = lax.axis_size(axis)
    copies = jnp.broadcast_to(v[None], (peers,) + v.shape)
    return jnp.sum(lax.all_to_all(copies, axis, 0, 0, tiled=False), axis=0)

def dft_tables(patch_len):
    index_row = jnp.arange(patch_len, dtype=jnp.int32)
    product = index_row[:, None] * index_row[None, :] % patch_len
    phase_angle = product.astype(jnp.float32) * (2.0 * math.pi / patch_len)
    return (jnp.cos(phase_angle).astype(jnp.bfloat16), jnp.sin(phase_angle).astype(jnp.bfloat16))


def conv_layers(rows_in, inside, conv1_w, conv1_b, conv2_w):
    sec_count = rows_in.shape[0]
    wide_rows = rows_in.shape[1] - 2
    strip_rows = wide_rows - 2
    patch_len = rows_in.shape[2]
    channels = conv1_w.shape[1]
    padded = jnp.pad(rows_in, ((0, 0), (0, 0), (1, 1)))
    layer_one = (
        jnp.zeros((sec_count, channels, wide_rows, patch_len), jnp.float32)
        + conv1_b[None, :, None, None]
    )
    for tap_row in range(3):
        for tap_col in range(3):
            weight_tap = conv1_w[3 * tap_row + tap_col].astype(jnp.float32)
            window = padded[:, tap_row : tap_row + wide_rows, tap_col : tap_col + patch_len].astype(
                jnp.float32
            )
            layer_one = layer_one + weight_tap[None, :, None, None] * window[:, None]
    hidden = jnp.where(inside[None, None, :, None], jax.nn.relu(layer_one), 0.0).astype(
        jnp.bfloat16
    )
    hidden_pad = jnp.pad(hidden, ((0, 0), (0, 0), (0, 0), (1, 1)))
    layer_two = jnp.zeros((sec_count, channels, strip_rows, patch_len), jnp.float32)
    for tap_row in range(3):
        for tap_col in range(3):
            window = hidden_pad[:, :, tap_row : tap_row + strip_rows, tap_col : tap_col + patch_len]
            layer_two = layer_two + jnp.einsum(
                "schw,co->sohw",
                window,
                conv2_w[3 * tap_row + tap_col],
                preferred_element_type=jnp.float32,
            )
    return layer_two.astype(jnp.bfloat16)


def patch_spectra(features, cosine, sin_table, rows_per):
    sec_count, channels, strip_rows, patch_len = features.shape
    patches = features.reshape(sec_count, channels, rows_per, patch_len, patch_len)
    patches = patches.transpose(0, 2, 1, 3, 4).reshape(-1, patch_len, patch_len)
    flat_rows = patches.reshape(-1, patch_len)
    half_cos = (
        jnp.dot(flat_rows, cosine, preferred_element_type=jnp.float32)
        .astype(jnp.bfloat16)
        .reshape(patches.shape)
    )
    half_sin = (
        jnp.dot(flat_rows, sin_table, preferred_element_type=jnp.float32)
        .astype(jnp.bfloat16)
        .reshape(patches.shape)
    )
    spec_real = jnp.einsum(
        "uy,byk->buk", cosine, half_cos, preferred_element_type=jnp.float32
    ) - jnp.einsum("uy,byk->buk", sin_table, half_sin, preferred_element_type=jnp.float32)
    spec_imag = -(
        jnp.einsum("uy,byk->buk", sin_table, half_cos, preferred_element_type=jnp.float32)
        + jnp.einsum("uy,byk->buk", cosine, half_sin, preferred_element_type=jnp.float32)
    )
    out_shape = (sec_count, rows_per, channels, patch_len, patch_len)
    return (
        spec_real.astype(jnp.bfloat16).reshape(out_shape),
        spec_imag.astype(jnp.bfloat16).reshape(out_shape),
    )


def correlate(own_real, own_imag, part_real, part_imag, pair_valid, cosine, sin_table):
    patch_len = own_real.shape[-1]
    channels = own_real.shape[2]
    own_re32 = own_real.astype(jnp.float32)
    own_im32 = own_imag.astype(jnp.float32)
    part_re32 = part_real.astype(jnp.float32)
    part_im32 = part_imag.astype(jnp.float32)
    freq_index = jnp.arange(patch_len, dtype=jnp.int32)
    zero_freq = (freq_index[:, None] == 0) & (freq_index[None, :] == 0)
    cross_real = jnp.sum(own_re32 * part_re32 + own_im32 * part_im32, axis=2).astype(jnp.bfloat16)
    cross_imag = jnp.sum(own_re32 * part_im32 - own_im32 * part_re32, axis=2).astype(jnp.bfloat16)
    drop = zero_freq[None, None] | ~pair_valid[:, None, None, None]
    cross_real = jnp.where(drop, jnp.zeros_like(cross_real), cross_real)
    cross_imag = jnp.where(drop, jnp.zeros_like(cross_imag), cross_imag)
    flat_real = cross_real.reshape(-1, patch_len)
    flat_imag = cross_imag.reshape(-1, patch_len)
    back_real = (
        jnp.dot(flat_real, cosine, preferred_element_type=jnp.float32)
        - jnp.dot(flat_imag, sin_table, preferred_element_type=jnp.float32)
    ).astype(jnp.bfloat16)
    back_imag = (
        jnp.dot(flat_real, sin_table, preferred_element_type=jnp.float32)
        + jnp.dot(flat_imag, cosine, preferred_element_type=jnp.float32)
    ).astype(jnp.bfloat16)
    back_real = back_real.reshape(-1, patch_len, patch_len)
    back_imag = back_imag.reshape(-1, patch_len, patch_len)
    raw_corr = jnp.einsum(
        "ju,buk->bjk", cosine, back_real, preferred_element_type=jnp.float32
    ) - jnp.einsum("ju,buk->bjk", sin_table, back_imag, preferred_element_type=jnp.float32)
    scores = raw_corr * (CORR_GAIN / (patch_len * patch_len * patch_len * math.sqrt(channels)))
    flat_scores = scores.reshape(-1, patch_len * patch_len)
    row_max = jnp.max(flat_scores, axis=1, keepdims=True)
    expos = jnp.exp(flat_scores - row_max)
    probability = expos / jnp.sum(expos, axis=1, keepdims=True)
    lag_index = jnp.arange(patch_len, dtype=jnp.int32)
    signed_lag = jnp.where(lag_index >= patch_len // 2, lag_index - patch_len, lag_index).astype(
        jnp.float32
    )
    lag_rows = jnp.broadcast_to(signed_lag[:, None], (patch_len, patch_len)).reshape(-1)
    lag_cols = jnp.broadcast_to(signed_lag[None, :], (patch_len, patch_len)).reshape(-1)
    flow_rows = jnp.sum(probability * lag_rows[None], axis=1) / FLOW_UNIT
    flow_cols = jnp.sum(probability * lag_cols[None], axis=1) / FLOW_UNIT
    return jnp.stack([flow_rows, flow_cols], axis=0)


def local(sections, offsets, valid_mask, conv1_w, conv1_b, conv2_w):
    sec_here = sections.shape[0]
    strip_rows = sections.shape[1]
    patch_len = sections.shape[2]
    rows_per = strip_rows // patch_len
    tile_count = lax.axis_size("tile")
    tile_pos = lax.axis_index("tile")
    cosine, sin_table = dft_tables(patch_len)
    padded_rows = with_halo(sections, (("tile", 1),), 2)
    next_rows = from_behind(padded_rows, "sec", -1)
    row_global = tile_pos * strip_rows - 1 + jnp.arange(strip_rows + 2, dtype=jnp.int32)
    inside = (row_global >= 0) & (row_global < strip_rows * tile_count)
    own_feats = conv_layers(padded_rows, inside, conv1_w, conv1_b, conv2_w)
    own_real, own_imag = patch_spectra(own_feats, cosine, sin_table, rows_per)
    next_feats = conv_layers(next_rows, inside, conv1_w, conv1_b, conv2_w)
    next_real, next_imag = patch_spectra(next_feats, cosine, sin_table, rows_per)
    combined_real = jnp.concatenate([own_real, next_real], axis=0)
    combined_imag = jnp.concatenate([own_imag, next_imag], axis=0)
    use_first = (offsets == 1)[:, None, None, None, None]
    part_real = jnp.where(
        use_first, combined_real[1 : sec_here + 1], combined_real[2 : sec_here + 2]
    )
    part_imag = jnp.where(
        use_first, combined_imag[1 : sec_here + 1], combined_imag[2 : sec_here + 2]
    )
    section_ids = lax.axis_index("sec") * sec_here + jnp.arange(sec_here, dtype=jnp.int32)
    total_sections = sec_here * lax.axis_size("sec")
    pair_valid = section_ids + offsets < total_sections
    flow_est = correlate(
        own_real, own_imag, part_real, part_imag, pair_valid, cosine, sin_table
    ).reshape(2, sec_here, rows_per)
    pair_ok = jnp.where(pair_valid, 1.0, 0.0).astype(jnp.float32)
    weights = valid_mask.astype(jnp.float32) * pair_ok[:, None]
    rows_all = rows_per * tile_count
    grid_y = (
        (tile_pos * rows_per + jnp.arange(rows_per, dtype=jnp.int32)).astype(jnp.float32) + 0.5
    ) / rows_all * 2.0 - 1.0
    weight_y = weights * grid_y[None]
    partial = jnp.concatenate(
        [
            jnp.sum(weights, axis=1)[:, None],
            jnp.sum(weight_y, axis=1)[:, None],
            jnp.sum(weight_y * grid_y[None], axis=1)[:, None],
            jnp.sum(flow_est * weights[None], axis=2).T,
            jnp.sum(flow_est * weight_y[None], axis=2).T,
        ],
        axis=1,
    )
    totals = tile_sum(partial, "tile")
    weight_sum, weighted_y, weighted_yy = totals[:, 0], totals[:, 1], totals[:, 2]
    flow_sum = totals[:, 3:5].T
    flow_y_sum = totals[:, 5:7].T
    m_zero = weight_sum + RIDGE_TERM
    m_two = weighted_yy + RIDGE_TERM
    determinant = m_zero * m_two - weighted_y * weighted_y
    offset_coef = (m_two[None] * flow_sum - weighted_y[None] * flow_y_sum) / determinant[None]
    slope_coef = (m_zero[None] * flow_y_sum - weighted_y[None] * flow_sum) / determinant[None]
    affine = jnp.stack([offset_coef[0], slope_coef[0], offset_coef[1], slope_coef[1]], axis=1)
    fitted = offset_coef[:, :, None] + slope_coef[:, :, None] * grid_y[None, None, :]
    residual = (flow_est - fitted) * weights[None]
    return (residual, affine)


def solution(mesh):
    placed = (P("sec", "tile", None), P("sec"), P("sec", "tile"), P(), P(), P())
    return jax.shard_map(
        local,
        mesh=mesh,
        in_specs=placed,
        out_specs=(P(None, "sec", "tile"), P("sec", None)),
        check_vma=False,
    )
```

```python
import math

import jax
import jax.numpy as jnp
from jax import lax
from jax.sharding import PartitionSpec as P

RIDGE_TERM = 1.0
CORR_GAIN = 2.5
FLOW_UNIT = 8.0


def with_halo(x, sides, width):
    for axis, dim in sides:
        peers, length = (lax.axis_size(axis), x.shape[dim])
        up = [(i, (i + 1) % peers) for i in range(peers - 1)]
        down = [(j, i) for i, j in up]
        last = lax.slice_in_dim(x, length - width, length, axis=dim)
        initial = lax.slice_in_dim(x, 0, width, axis=dim)
        before = lax.ppermute(last, axis, up)
        after = lax.ppermute(initial, axis, down)
        x = jnp.concatenate([before, x, after], axis=dim)
    return x


def from_behind(block, axis, distance):
    devices = range(lax.axis_size(axis))
    route = [(i - distance, i) for i in devices if i - distance in devices]
    return lax.ppermute(block, axis, route)


def tile_sum(v, axis):
    peers = lax.axis_size(axis)
    copies = jnp.broadcast_to(v[None], (peers,) + v.shape)
    return jnp.sum(lax.all_to_all(copies, axis, 0, 0, tiled=False), axis=0)

def dft_tables(patch_len):
    index_row = jnp.arange(patch_len, dtype=jnp.int32)
    product = index_row[:, None] * index_row[None, :] % patch_len
    phase_angle = product.astype(jnp.float32) * (2.0 * math.pi / patch_len)
    return (jnp.cos(phase_angle).astype(jnp.bfloat16), jnp.sin(phase_angle).astype(jnp.bfloat16))


def conv_layers(rows_in, inside, conv1_w, conv1_b, conv2_w):
    sec_count = rows_in.shape[0]
    wide_rows = rows_in.shape[1] - 2
    strip_rows = wide_rows - 2
    patch_len = rows_in.shape[2]
    channels = conv1_w.shape[1]
    padded = jnp.pad(rows_in, ((0, 0), (0, 0), (1, 1)))
    layer_one = (
        jnp.zeros((sec_count, channels, wide_rows, patch_len), jnp.float32)
        + conv1_b[None, :, None, None]
    )
    for tap_row in range(3):
        for tap_col in range(3):
            weight_tap = conv1_w[3 * tap_row + tap_col].astype(jnp.float32)
            window = padded[:, tap_row : tap_row + wide_rows, tap_col : tap_col + patch_len].astype(
                jnp.float32
            )
            layer_one = layer_one + weight_tap[None, :, None, None] * window[:, None]
    hidden = jnp.where(inside[None, None, :, None], jax.nn.relu(layer_one), 0.0).astype(
        jnp.bfloat16
    )
    hidden_pad = jnp.pad(hidden, ((0, 0), (0, 0), (0, 0), (1, 1)))
    layer_two = jnp.zeros((sec_count, channels, strip_rows, patch_len), jnp.float32)
    for tap_row in range(3):
        for tap_col in range(3):
            window = hidden_pad[:, :, tap_row : tap_row + strip_rows, tap_col : tap_col + patch_len]
            layer_two = layer_two + jnp.einsum(
                "schw,co->sohw",
                window,
                conv2_w[3 * tap_row + tap_col],
                preferred_element_type=jnp.float32,
            )
    return layer_two.astype(jnp.bfloat16)


def patch_spectra(features, cosine, sin_table, rows_per):
    sec_count, channels, strip_rows, patch_len = features.shape
    patches = features.reshape(sec_count, channels, rows_per, patch_len, patch_len)
    patches = patches.transpose(0, 2, 1, 3, 4).reshape(-1, patch_len, patch_len)
    flat_rows = patches.reshape(-1, patch_len)
    half_both = jnp.dot(
        flat_rows, jnp.concatenate([cosine, sin_table], axis=1), preferred_element_type=jnp.float32
    ).astype(jnp.bfloat16)
    half_cos = half_both[:, :patch_len].reshape(patches.shape)
    half_sin = half_both[:, patch_len:].reshape(patches.shape)
    left_cos = jnp.concatenate([cosine, -sin_table], axis=0)
    left_sin = jnp.concatenate([-sin_table, -cosine], axis=0)
    spec_both = jnp.einsum(
        "uy,byk->buk", left_cos, half_cos, preferred_element_type=jnp.float32
    ) + jnp.einsum("uy,byk->buk", left_sin, half_sin, preferred_element_type=jnp.float32)
    spec_both = spec_both.astype(jnp.bfloat16)
    spec_real = spec_both[:, :patch_len]
    spec_imag = spec_both[:, patch_len:]
    out_shape = (sec_count, rows_per, channels, patch_len, patch_len)
    return (
        spec_real.reshape(out_shape),
        spec_imag.reshape(out_shape),
    )


def correlate(own_real, own_imag, part_real, part_imag, pair_valid, cosine, sin_table):
    patch_len = own_real.shape[-1]
    channels = own_real.shape[2]
    own_re32 = own_real.astype(jnp.float32)
    own_im32 = own_imag.astype(jnp.float32)
    part_re32 = part_real.astype(jnp.float32)
    part_im32 = part_imag.astype(jnp.float32)
    freq_index = jnp.arange(patch_len, dtype=jnp.int32)
    zero_freq = (freq_index[:, None] == 0) & (freq_index[None, :] == 0)
    cross_real = jnp.sum(own_re32 * part_re32 + own_im32 * part_im32, axis=2).astype(jnp.bfloat16)
    cross_imag = jnp.sum(own_re32 * part_im32 - own_im32 * part_re32, axis=2).astype(jnp.bfloat16)
    drop = zero_freq[None, None] | ~pair_valid[:, None, None, None]
    cross_real = jnp.where(drop, jnp.zeros_like(cross_real), cross_real)
    cross_imag = jnp.where(drop, jnp.zeros_like(cross_imag), cross_imag)
    flat_real = cross_real.reshape(-1, patch_len)
    flat_imag = cross_imag.reshape(-1, patch_len)
    back_both = (
        jnp.dot(
            flat_real,
            jnp.concatenate([cosine, sin_table], axis=1),
            preferred_element_type=jnp.float32,
        )
        + jnp.dot(
            flat_imag,
            jnp.concatenate([-sin_table, cosine], axis=1),
            preferred_element_type=jnp.float32,
        )
    ).astype(jnp.bfloat16)
    back_real = back_both[:, :patch_len]
    back_imag = back_both[:, patch_len:]
    back_real = back_real.reshape(-1, patch_len, patch_len)
    back_imag = back_imag.reshape(-1, patch_len, patch_len)
    raw_corr = jnp.einsum(
        "ju,buk->bjk", cosine, back_real, preferred_element_type=jnp.float32
    ) - jnp.einsum("ju,buk->bjk", sin_table, back_imag, preferred_element_type=jnp.float32)
    scores = raw_corr * (CORR_GAIN / (patch_len * patch_len * patch_len * math.sqrt(channels)))
    flat_scores = scores.reshape(-1, patch_len * patch_len)
    row_max = jnp.max(flat_scores, axis=1, keepdims=True)
    expos = jnp.exp(flat_scores - row_max)
    probability = expos / jnp.sum(expos, axis=1, keepdims=True)
    lag_index = jnp.arange(patch_len, dtype=jnp.int32)
    signed_lag = jnp.where(lag_index >= patch_len // 2, lag_index - patch_len, lag_index).astype(
        jnp.float32
    )
    lag_rows = jnp.broadcast_to(signed_lag[:, None], (patch_len, patch_len)).reshape(-1)
    lag_cols = jnp.broadcast_to(signed_lag[None, :], (patch_len, patch_len)).reshape(-1)
    flow_rows = jnp.sum(probability * lag_rows[None], axis=1) / FLOW_UNIT
    flow_cols = jnp.sum(probability * lag_cols[None], axis=1) / FLOW_UNIT
    return jnp.stack([flow_rows, flow_cols], axis=0)


def local(sections, offsets, valid_mask, conv1_w, conv1_b, conv2_w):
    sec_here = sections.shape[0]
    strip_rows = sections.shape[1]
    patch_len = sections.shape[2]
    rows_per = strip_rows // patch_len
    tile_count = lax.axis_size("tile")
    tile_pos = lax.axis_index("tile")
    cosine, sin_table = dft_tables(patch_len)
    padded_rows = with_halo(sections, (("tile", 1),), 2)
    next_rows = from_behind(padded_rows, "sec", -1)
    row_global = tile_pos * strip_rows - 1 + jnp.arange(strip_rows + 2, dtype=jnp.int32)
    inside = (row_global >= 0) & (row_global < strip_rows * tile_count)
    own_feats = conv_layers(padded_rows, inside, conv1_w, conv1_b, conv2_w)
    own_real, own_imag = patch_spectra(own_feats, cosine, sin_table, rows_per)
    next_feats = conv_layers(next_rows, inside, conv1_w, conv1_b, conv2_w)
    next_real, next_imag = patch_spectra(next_feats, cosine, sin_table, rows_per)
    combined_real = jnp.concatenate([own_real, next_real], axis=0)
    combined_imag = jnp.concatenate([own_imag, next_imag], axis=0)
    use_first = (offsets == 1)[:, None, None, None, None]
    part_real = jnp.where(
        use_first, combined_real[1 : sec_here + 1], combined_real[2 : sec_here + 2]
    )
    part_imag = jnp.where(
        use_first, combined_imag[1 : sec_here + 1], combined_imag[2 : sec_here + 2]
    )
    section_ids = lax.axis_index("sec") * sec_here + jnp.arange(sec_here, dtype=jnp.int32)
    total_sections = sec_here * lax.axis_size("sec")
    pair_valid = section_ids + offsets < total_sections
    flow_est = correlate(
        own_real, own_imag, part_real, part_imag, pair_valid, cosine, sin_table
    ).reshape(2, sec_here, rows_per)
    pair_ok = jnp.where(pair_valid, 1.0, 0.0).astype(jnp.float32)
    weights = valid_mask.astype(jnp.float32) * pair_ok[:, None]
    rows_all = rows_per * tile_count
    grid_y = (
        (tile_pos * rows_per + jnp.arange(rows_per, dtype=jnp.int32)).astype(jnp.float32) + 0.5
    ) / rows_all * 2.0 - 1.0
    weight_y = weights * grid_y[None]
    partial = jnp.concatenate(
        [
            jnp.sum(weights, axis=1)[:, None],
            jnp.sum(weight_y, axis=1)[:, None],
            jnp.sum(weight_y * grid_y[None], axis=1)[:, None],
            jnp.sum(flow_est * weights[None], axis=2).T,
            jnp.sum(flow_est * weight_y[None], axis=2).T,
        ],
        axis=1,
    )
    totals = tile_sum(partial, "tile")
    weight_sum, weighted_y, weighted_yy = totals[:, 0], totals[:, 1], totals[:, 2]
    flow_sum = totals[:, 3:5].T
    flow_y_sum = totals[:, 5:7].T
    m_zero = weight_sum + RIDGE_TERM
    m_two = weighted_yy + RIDGE_TERM
    determinant = m_zero * m_two - weighted_y * weighted_y
    offset_coef = (m_two[None] * flow_sum - weighted_y[None] * flow_y_sum) / determinant[None]
    slope_coef = (m_zero[None] * flow_y_sum - weighted_y[None] * flow_sum) / determinant[None]
    affine = jnp.stack([offset_coef[0], slope_coef[0], offset_coef[1], slope_coef[1]], axis=1)
    fitted = offset_coef[:, :, None] + slope_coef[:, :, None] * grid_y[None, None, :]
    residual = (flow_est - fitted) * weights[None]
    return (residual, affine)


def solution(mesh):
    placed = (P("sec", "tile", None), P("sec"), P("sec", "tile"), P(), P(), P())
    return jax.shard_map(
        local,
        mesh=mesh,
        in_specs=placed,
        out_specs=(P(None, "sec", "tile"), P("sec", None)),
        check_vma=False,
    )
```

```python
import math

import jax
import jax.numpy as jnp
from jax import lax
from jax.sharding import PartitionSpec as P

RIDGE_TERM = 1.0
CORR_GAIN = 2.5
FLOW_UNIT = 8.0


def with_halo(x, sides, width):
    for axis, dim in sides:
        peers, length = (lax.axis_size(axis), x.shape[dim])
        up = [(i, (i + 1) % peers) for i in range(peers - 1)]
        down = [(j, i) for i, j in up]
        last = lax.slice_in_dim(x, length - width, length, axis=dim)
        initial = lax.slice_in_dim(x, 0, width, axis=dim)
        before = lax.ppermute(last, axis, up)
        after = lax.ppermute(initial, axis, down)
        x = jnp.concatenate([before, x, after], axis=dim)
    return x


def from_behind(block, axis, distance):
    devices = range(lax.axis_size(axis))
    route = [(i - distance, i) for i in devices if i - distance in devices]
    return lax.ppermute(block, axis, route)


def tile_sum(v, axis):
    peers = lax.axis_size(axis)
    copies = jnp.broadcast_to(v[None], (peers,) + v.shape)
    return jnp.sum(lax.all_to_all(copies, axis, 0, 0, tiled=False), axis=0)

def dft_tables(patch_len):
    index_row = jnp.arange(patch_len, dtype=jnp.int32)
    product = index_row[:, None] * index_row[None, :] % patch_len
    phase_angle = product.astype(jnp.float32) * (2.0 * math.pi / patch_len)
    return (jnp.cos(phase_angle).astype(jnp.bfloat16), jnp.sin(phase_angle).astype(jnp.bfloat16))


def conv_layers(rows_in, inside, conv1_w, conv1_b, conv2_w):
    sec_count = rows_in.shape[0]
    wide_rows = rows_in.shape[1] - 2
    strip_rows = wide_rows - 2
    patch_len = rows_in.shape[2]
    channels = conv1_w.shape[1]
    padded = jnp.pad(rows_in, ((0, 0), (0, 0), (1, 1)))
    layer_one = (
        jnp.zeros((sec_count, channels, wide_rows, patch_len), jnp.float32)
        + conv1_b[None, :, None, None]
    )
    for tap_row in range(3):
        for tap_col in range(3):
            weight_tap = conv1_w[3 * tap_row + tap_col].astype(jnp.float32)
            window = padded[:, tap_row : tap_row + wide_rows, tap_col : tap_col + patch_len].astype(
                jnp.float32
            )
            layer_one = layer_one + weight_tap[None, :, None, None] * window[:, None]
    hidden = jnp.where(inside[None, None, :, None], jax.nn.relu(layer_one), 0.0).astype(
        jnp.bfloat16
    )
    hidden_pad = jnp.pad(hidden, ((0, 0), (0, 0), (0, 0), (1, 1)))
    layer_two = jnp.zeros((sec_count, channels, strip_rows, patch_len), jnp.float32)
    for tap_row in range(3):
        for tap_col in range(3):
            window = hidden_pad[:, :, tap_row : tap_row + strip_rows, tap_col : tap_col + patch_len]
            layer_two = layer_two + jnp.einsum(
                "schw,co->sohw",
                window,
                conv2_w[3 * tap_row + tap_col],
                preferred_element_type=jnp.float32,
            )
    return layer_two.astype(jnp.bfloat16)


def patch_spectra(features, cosine, sin_table, rows_per):
    sec_count, channels, strip_rows, patch_len = features.shape
    patches = features.reshape(sec_count, channels, rows_per, patch_len, patch_len)
    patches = patches.transpose(0, 2, 1, 3, 4).reshape(-1, patch_len, patch_len)
    flat_rows = patches.reshape(-1, patch_len)
    half_both = jnp.dot(
        flat_rows, jnp.concatenate([cosine, sin_table], axis=1), preferred_element_type=jnp.float32
    ).astype(jnp.bfloat16)
    half_cos = half_both[:, :patch_len].reshape(patches.shape)
    half_sin = half_both[:, patch_len:].reshape(patches.shape)
    left_cos = jnp.concatenate([cosine, -sin_table], axis=0)
    left_sin = jnp.concatenate([-sin_table, -cosine], axis=0)
    spec_both = jnp.einsum(
        "uy,byk->buk", left_cos, half_cos, preferred_element_type=jnp.float32
    ) + jnp.einsum("uy,byk->buk", left_sin, half_sin, preferred_element_type=jnp.float32)
    spec_both = spec_both.astype(jnp.bfloat16)
    spec_real = spec_both[:, :patch_len]
    spec_imag = spec_both[:, patch_len:]
    out_shape = (sec_count, rows_per, channels, patch_len, patch_len)
    return (
        spec_real.reshape(out_shape),
        spec_imag.reshape(out_shape),
    )


def correlate(own_real, own_imag, part_real, part_imag, pair_valid, cosine, sin_table):
    patch_len = own_real.shape[-1]
    channels = own_real.shape[2]
    own_re32 = own_real.astype(jnp.float32)
    own_im32 = own_imag.astype(jnp.float32)
    part_re32 = part_real.astype(jnp.float32)
    part_im32 = part_imag.astype(jnp.float32)
    freq_index = jnp.arange(patch_len, dtype=jnp.int32)
    zero_freq = (freq_index[:, None] == 0) & (freq_index[None, :] == 0)
    cross_real = jnp.sum(own_re32 * part_re32 + own_im32 * part_im32, axis=2).astype(jnp.bfloat16)
    cross_imag = jnp.sum(own_re32 * part_im32 - own_im32 * part_re32, axis=2).astype(jnp.bfloat16)
    drop = zero_freq[None, None] | ~pair_valid[:, None, None, None]
    cross_real = jnp.where(drop, jnp.zeros_like(cross_real), cross_real)
    cross_imag = jnp.where(drop, jnp.zeros_like(cross_imag), cross_imag)
    flat_real = cross_real.reshape(-1, patch_len)
    flat_imag = cross_imag.reshape(-1, patch_len)
    back_both = (
        jnp.dot(
            flat_real,
            jnp.concatenate([cosine, sin_table], axis=1),
            preferred_element_type=jnp.float32,
        )
        + jnp.dot(
            flat_imag,
            jnp.concatenate([-sin_table, cosine], axis=1),
            preferred_element_type=jnp.float32,
        )
    ).astype(jnp.bfloat16)
    back_real = back_both[:, :patch_len]
    back_imag = back_both[:, patch_len:]
    back_real = back_real.reshape(-1, patch_len, patch_len)
    back_imag = back_imag.reshape(-1, patch_len, patch_len)
    raw_corr = jnp.einsum(
        "ju,buk->bjk", cosine, back_real, preferred_element_type=jnp.float32
    ) - jnp.einsum("ju,buk->bjk", sin_table, back_imag, preferred_element_type=jnp.float32)
    scores = raw_corr * (CORR_GAIN / (patch_len * patch_len * patch_len * math.sqrt(channels)))
    flat_scores = scores.reshape(-1, patch_len * patch_len)
    row_max = jnp.max(flat_scores, axis=1, keepdims=True)
    expos = jnp.exp(flat_scores - row_max)
    probability = expos / jnp.sum(expos, axis=1, keepdims=True)
    lag_index = jnp.arange(patch_len, dtype=jnp.int32)
    signed_lag = jnp.where(lag_index >= patch_len // 2, lag_index - patch_len, lag_index).astype(
        jnp.float32
    )
    lag_rows = jnp.broadcast_to(signed_lag[:, None], (patch_len, patch_len)).reshape(-1)
    lag_cols = jnp.broadcast_to(signed_lag[None, :], (patch_len, patch_len)).reshape(-1)
    flow_rows = jnp.sum(probability * lag_rows[None], axis=1) / FLOW_UNIT
    flow_cols = jnp.sum(probability * lag_cols[None], axis=1) / FLOW_UNIT
    return jnp.stack([flow_rows, flow_cols], axis=0)


def local(sections, offsets, valid_mask, conv1_w, conv1_b, conv2_w):
    sec_here = sections.shape[0]
    strip_rows = sections.shape[1]
    patch_len = sections.shape[2]
    rows_per = strip_rows // patch_len
    tile_count = lax.axis_size("tile")
    tile_pos = lax.axis_index("tile")
    cosine, sin_table = dft_tables(patch_len)
    padded_rows = with_halo(sections, (("tile", 1),), 2)
    row_global = tile_pos * strip_rows - 1 + jnp.arange(strip_rows + 2, dtype=jnp.int32)
    inside = (row_global >= 0) & (row_global < strip_rows * tile_count)
    own_feats = conv_layers(padded_rows, inside, conv1_w, conv1_b, conv2_w)
    own_feats, rows_out = lax.optimization_barrier((own_feats, padded_rows))
    next_rows = from_behind(rows_out, "sec", -1)
    own_real, own_imag = patch_spectra(own_feats, cosine, sin_table, rows_per)
    next_feats = conv_layers(next_rows, inside, conv1_w, conv1_b, conv2_w)
    next_real, next_imag = patch_spectra(next_feats, cosine, sin_table, rows_per)
    combined_real = jnp.concatenate([own_real, next_real], axis=0)
    combined_imag = jnp.concatenate([own_imag, next_imag], axis=0)
    use_first = (offsets == 1)[:, None, None, None, None]
    part_real = jnp.where(
        use_first, combined_real[1 : sec_here + 1], combined_real[2 : sec_here + 2]
    )
    part_imag = jnp.where(
        use_first, combined_imag[1 : sec_here + 1], combined_imag[2 : sec_here + 2]
    )
    section_ids = lax.axis_index("sec") * sec_here + jnp.arange(sec_here, dtype=jnp.int32)
    total_sections = sec_here * lax.axis_size("sec")
    pair_valid = section_ids + offsets < total_sections
    flow_est = correlate(
        own_real, own_imag, part_real, part_imag, pair_valid, cosine, sin_table
    ).reshape(2, sec_here, rows_per)
    pair_ok = jnp.where(pair_valid, 1.0, 0.0).astype(jnp.float32)
    weights = valid_mask.astype(jnp.float32) * pair_ok[:, None]
    rows_all = rows_per * tile_count
    grid_y = (
        (tile_pos * rows_per + jnp.arange(rows_per, dtype=jnp.int32)).astype(jnp.float32) + 0.5
    ) / rows_all * 2.0 - 1.0
    weight_y = weights * grid_y[None]
    partial = jnp.concatenate(
        [
            jnp.sum(weights, axis=1)[:, None],
            jnp.sum(weight_y, axis=1)[:, None],
            jnp.sum(weight_y * grid_y[None], axis=1)[:, None],
            jnp.sum(flow_est * weights[None], axis=2).T,
            jnp.sum(flow_est * weight_y[None], axis=2).T,
        ],
        axis=1,
    )
    totals = tile_sum(partial, "tile")
    weight_sum, weighted_y, weighted_yy = totals[:, 0], totals[:, 1], totals[:, 2]
    flow_sum = totals[:, 3:5].T
    flow_y_sum = totals[:, 5:7].T
    m_zero = weight_sum + RIDGE_TERM
    m_two = weighted_yy + RIDGE_TERM
    determinant = m_zero * m_two - weighted_y * weighted_y
    offset_coef = (m_two[None] * flow_sum - weighted_y[None] * flow_y_sum) / determinant[None]
    slope_coef = (m_zero[None] * flow_y_sum - weighted_y[None] * flow_sum) / determinant[None]
    affine = jnp.stack([offset_coef[0], slope_coef[0], offset_coef[1], slope_coef[1]], axis=1)
    fitted = offset_coef[:, :, None] + slope_coef[:, :, None] * grid_y[None, None, :]
    residual = (flow_est - fitted) * weights[None]
    return (residual, affine)


def solution(mesh):
    placed = (P("sec", "tile", None), P("sec"), P("sec", "tile"), P(), P(), P())
    return jax.shard_map(
        local,
        mesh=mesh,
        in_specs=placed,
        out_specs=(P(None, "sec", "tile"), P("sec", None)),
        check_vma=False,
    )
```

```python
import math

import jax
import jax.numpy as jnp
from jax import lax
from jax.sharding import PartitionSpec as P

RIDGE_TERM = 1.0
CORR_GAIN = 2.5
FLOW_UNIT = 8.0


def with_halo(x, sides, width):
    for axis, dim in sides:
        peers, length = (lax.axis_size(axis), x.shape[dim])
        up = [(i, (i + 1) % peers) for i in range(peers - 1)]
        down = [(j, i) for i, j in up]
        last = lax.slice_in_dim(x, length - width, length, axis=dim)
        initial = lax.slice_in_dim(x, 0, width, axis=dim)
        before = lax.ppermute(last, axis, up)
        after = lax.ppermute(initial, axis, down)
        x = jnp.concatenate([before, x, after], axis=dim)
    return x


def from_behind(block, axis, distance):
    devices = range(lax.axis_size(axis))
    route = [(i - distance, i) for i in devices if i - distance in devices]
    return lax.ppermute(block, axis, route)


def tile_sum(v, axis):
    peers = lax.axis_size(axis)
    copies = jnp.broadcast_to(v[None], (peers,) + v.shape)
    return jnp.sum(lax.all_to_all(copies, axis, 0, 0, tiled=False), axis=0)

def dft_tables(patch_len):
    index_row = jnp.arange(patch_len, dtype=jnp.int32)
    product = index_row[:, None] * index_row[None, :] % patch_len
    phase_angle = product.astype(jnp.float32) * (2.0 * math.pi / patch_len)
    return (jnp.cos(phase_angle).astype(jnp.bfloat16), jnp.sin(phase_angle).astype(jnp.bfloat16))


def conv_one(rows_in, inside, conv1_w, conv1_b):
    sec_count = rows_in.shape[0]
    wide_rows = rows_in.shape[1] - 2
    strip_rows = wide_rows - 2
    patch_len = rows_in.shape[2]
    channels = conv1_w.shape[1]
    padded = jnp.pad(rows_in, ((0, 0), (0, 0), (1, 1)))
    layer_one = (
        jnp.zeros((sec_count, channels, wide_rows, patch_len), jnp.float32)
        + conv1_b[None, :, None, None]
    )
    for tap_row in range(3):
        for tap_col in range(3):
            weight_tap = conv1_w[3 * tap_row + tap_col].astype(jnp.float32)
            window = padded[:, tap_row : tap_row + wide_rows, tap_col : tap_col + patch_len].astype(
                jnp.float32
            )
            layer_one = layer_one + weight_tap[None, :, None, None] * window[:, None]
    hidden = jnp.where(inside[None, None, :, None], jax.nn.relu(layer_one), 0.0).astype(
        jnp.bfloat16
    )
    return hidden


def conv_two(hidden, conv2_w):
    sec_count, channels, wide_rows, patch_len = hidden.shape
    strip_rows = wide_rows - 2
    hidden_pad = jnp.pad(hidden, ((0, 0), (0, 0), (0, 0), (1, 1)))
    layer_two = jnp.zeros((sec_count, channels, strip_rows, patch_len), jnp.float32)
    for tap_row in range(3):
        for tap_col in range(3):
            window = hidden_pad[:, :, tap_row : tap_row + strip_rows, tap_col : tap_col + patch_len]
            layer_two = layer_two + jnp.einsum(
                "schw,co->sohw",
                window,
                conv2_w[3 * tap_row + tap_col],
                preferred_element_type=jnp.float32,
            )
    return layer_two.astype(jnp.bfloat16)


def patch_spectra(features, cosine, sin_table, rows_per):
    sec_count, channels, strip_rows, patch_len = features.shape
    patches = features.reshape(sec_count, channels, rows_per, patch_len, patch_len)
    patches = patches.transpose(0, 2, 1, 3, 4).reshape(-1, patch_len, patch_len)
    flat_rows = patches.reshape(-1, patch_len)
    half_both = jnp.dot(
        flat_rows, jnp.concatenate([cosine, sin_table], axis=1), preferred_element_type=jnp.float32
    ).astype(jnp.bfloat16)
    half_cos = half_both[:, :patch_len].reshape(patches.shape)
    half_sin = half_both[:, patch_len:].reshape(patches.shape)
    left_cos = jnp.concatenate([cosine, -sin_table], axis=0)
    left_sin = jnp.concatenate([-sin_table, -cosine], axis=0)
    spec_both = jnp.einsum(
        "uy,byk->buk", left_cos, half_cos, preferred_element_type=jnp.float32
    ) + jnp.einsum("uy,byk->buk", left_sin, half_sin, preferred_element_type=jnp.float32)
    spec_both = spec_both.astype(jnp.bfloat16)
    spec_real = spec_both[:, :patch_len]
    spec_imag = spec_both[:, patch_len:]
    out_shape = (sec_count, rows_per, channels, patch_len, patch_len)
    return (
        spec_real.reshape(out_shape),
        spec_imag.reshape(out_shape),
    )


def correlate(own_real, own_imag, part_real, part_imag, pair_valid, cosine, sin_table):
    patch_len = own_real.shape[-1]
    channels = own_real.shape[2]
    own_re32 = own_real.astype(jnp.float32)
    own_im32 = own_imag.astype(jnp.float32)
    part_re32 = part_real.astype(jnp.float32)
    part_im32 = part_imag.astype(jnp.float32)
    freq_index = jnp.arange(patch_len, dtype=jnp.int32)
    zero_freq = (freq_index[:, None] == 0) & (freq_index[None, :] == 0)
    cross_real = jnp.sum(own_re32 * part_re32 + own_im32 * part_im32, axis=2).astype(jnp.bfloat16)
    cross_imag = jnp.sum(own_re32 * part_im32 - own_im32 * part_re32, axis=2).astype(jnp.bfloat16)
    drop = zero_freq[None, None] | ~pair_valid[:, None, None, None]
    cross_real = jnp.where(drop, jnp.zeros_like(cross_real), cross_real)
    cross_imag = jnp.where(drop, jnp.zeros_like(cross_imag), cross_imag)
    flat_real = cross_real.reshape(-1, patch_len)
    flat_imag = cross_imag.reshape(-1, patch_len)
    back_both = (
        jnp.dot(
            flat_real,
            jnp.concatenate([cosine, sin_table], axis=1),
            preferred_element_type=jnp.float32,
        )
        + jnp.dot(
            flat_imag,
            jnp.concatenate([-sin_table, cosine], axis=1),
            preferred_element_type=jnp.float32,
        )
    ).astype(jnp.bfloat16)
    back_real = back_both[:, :patch_len]
    back_imag = back_both[:, patch_len:]
    back_real = back_real.reshape(-1, patch_len, patch_len)
    back_imag = back_imag.reshape(-1, patch_len, patch_len)
    raw_corr = jnp.einsum(
        "ju,buk->bjk", cosine, back_real, preferred_element_type=jnp.float32
    ) - jnp.einsum("ju,buk->bjk", sin_table, back_imag, preferred_element_type=jnp.float32)
    scores = raw_corr * (CORR_GAIN / (patch_len * patch_len * patch_len * math.sqrt(channels)))
    flat_scores = scores.reshape(-1, patch_len * patch_len)
    row_max = jnp.max(flat_scores, axis=1, keepdims=True)
    expos = jnp.exp(flat_scores - row_max)
    probability = expos / jnp.sum(expos, axis=1, keepdims=True)
    lag_index = jnp.arange(patch_len, dtype=jnp.int32)
    signed_lag = jnp.where(lag_index >= patch_len // 2, lag_index - patch_len, lag_index).astype(
        jnp.float32
    )
    lag_rows = jnp.broadcast_to(signed_lag[:, None], (patch_len, patch_len)).reshape(-1)
    lag_cols = jnp.broadcast_to(signed_lag[None, :], (patch_len, patch_len)).reshape(-1)
    flow_rows = jnp.sum(probability * lag_rows[None], axis=1) / FLOW_UNIT
    flow_cols = jnp.sum(probability * lag_cols[None], axis=1) / FLOW_UNIT
    return jnp.stack([flow_rows, flow_cols], axis=0)


def local(sections, offsets, valid_mask, conv1_w, conv1_b, conv2_w):
    sec_here = sections.shape[0]
    strip_rows = sections.shape[1]
    patch_len = sections.shape[2]
    rows_per = strip_rows // patch_len
    tile_count = lax.axis_size("tile")
    tile_pos = lax.axis_index("tile")
    cosine, sin_table = dft_tables(patch_len)
    next_raw = from_behind(sections, "sec", -1)
    padded_rows = with_halo(jnp.concatenate([sections, next_raw], axis=0), (("tile", 1),), 2)
    row_global = tile_pos * strip_rows - 1 + jnp.arange(strip_rows + 2, dtype=jnp.int32)
    inside = (row_global >= 0) & (row_global < strip_rows * tile_count)
    hidden_all = conv_one(padded_rows, inside, conv1_w, conv1_b)
    own_feats = conv_two(hidden_all[:sec_here], conv2_w)
    own_real, own_imag = patch_spectra(own_feats, cosine, sin_table, rows_per)
    next_feats = conv_two(hidden_all[sec_here:], conv2_w)
    next_real, next_imag = patch_spectra(next_feats, cosine, sin_table, rows_per)
    combined_real = jnp.concatenate([own_real, next_real], axis=0)
    combined_imag = jnp.concatenate([own_imag, next_imag], axis=0)
    use_first = (offsets == 1)[:, None, None, None, None]
    part_real = jnp.where(
        use_first, combined_real[1 : sec_here + 1], combined_real[2 : sec_here + 2]
    )
    part_imag = jnp.where(
        use_first, combined_imag[1 : sec_here + 1], combined_imag[2 : sec_here + 2]
    )
    section_ids = lax.axis_index("sec") * sec_here + jnp.arange(sec_here, dtype=jnp.int32)
    total_sections = sec_here * lax.axis_size("sec")
    pair_valid = section_ids + offsets < total_sections
    flow_est = correlate(
        own_real, own_imag, part_real, part_imag, pair_valid, cosine, sin_table
    ).reshape(2, sec_here, rows_per)
    pair_ok = jnp.where(pair_valid, 1.0, 0.0).astype(jnp.float32)
    weights = valid_mask.astype(jnp.float32) * pair_ok[:, None]
    rows_all = rows_per * tile_count
    grid_y = (
        (tile_pos * rows_per + jnp.arange(rows_per, dtype=jnp.int32)).astype(jnp.float32) + 0.5
    ) / rows_all * 2.0 - 1.0
    weight_y = weights * grid_y[None]
    partial = jnp.concatenate(
        [
            jnp.sum(weights, axis=1)[:, None],
            jnp.sum(weight_y, axis=1)[:, None],
            jnp.sum(weight_y * grid_y[None], axis=1)[:, None],
            jnp.sum(flow_est * weights[None], axis=2).T,
            jnp.sum(flow_est * weight_y[None], axis=2).T,
        ],
        axis=1,
    )
    totals = tile_sum(partial, "tile")
    weight_sum, weighted_y, weighted_yy = totals[:, 0], totals[:, 1], totals[:, 2]
    flow_sum = totals[:, 3:5].T
    flow_y_sum = totals[:, 5:7].T
    m_zero = weight_sum + RIDGE_TERM
    m_two = weighted_yy + RIDGE_TERM
    determinant = m_zero * m_two - weighted_y * weighted_y
    offset_coef = (m_two[None] * flow_sum - weighted_y[None] * flow_y_sum) / determinant[None]
    slope_coef = (m_zero[None] * flow_y_sum - weighted_y[None] * flow_sum) / determinant[None]
    affine = jnp.stack([offset_coef[0], slope_coef[0], offset_coef[1], slope_coef[1]], axis=1)
    fitted = offset_coef[:, :, None] + slope_coef[:, :, None] * grid_y[None, None, :]
    residual = (flow_est - fitted) * weights[None]
    return (residual, affine)


def solution(mesh):
    placed = (P("sec", "tile", None), P("sec"), P("sec", "tile"), P(), P(), P())
    return jax.shard_map(
        local,
        mesh=mesh,
        in_specs=placed,
        out_specs=(P(None, "sec", "tile"), P("sec", None)),
        check_vma=False,
    )
```

```python
import math

import jax
import jax.numpy as jnp
from jax import lax
from jax.sharding import PartitionSpec as P
from jax.experimental import pallas as pl
from jax.experimental.pallas import tpu as pltpu

RIDGE_TERM = 1.0
CORR_GAIN = 2.5
FLOW_UNIT = 8.0


def with_halo(x, sides, width):
    for axis, dim in sides:
        peers, length = (lax.axis_size(axis), x.shape[dim])
        up = [(i, (i + 1) % peers) for i in range(peers - 1)]
        down = [(j, i) for i, j in up]
        last = lax.slice_in_dim(x, length - width, length, axis=dim)
        initial = lax.slice_in_dim(x, 0, width, axis=dim)
        before = lax.ppermute(last, axis, up)
        after = lax.ppermute(initial, axis, down)
        x = jnp.concatenate([before, x, after], axis=dim)
    return x


def from_behind(block, axis, distance):
    devices = range(lax.axis_size(axis))
    route = [(i - distance, i) for i in devices if i - distance in devices]
    return lax.ppermute(block, axis, route)


def tile_sum(v, axis):
    peers = lax.axis_size(axis)
    copies = jnp.broadcast_to(v[None], (peers,) + v.shape)
    return jnp.sum(lax.all_to_all(copies, axis, 0, 0, tiled=False), axis=0)

def dft_tables(patch_len):
    index_row = jnp.arange(patch_len, dtype=jnp.int32)
    product = index_row[:, None] * index_row[None, :] % patch_len
    phase_angle = product.astype(jnp.float32) * (2.0 * math.pi / patch_len)
    return (jnp.cos(phase_angle).astype(jnp.bfloat16), jnp.sin(phase_angle).astype(jnp.bfloat16))


def conv_one_kernel(w_ref, b_ref, keep_ref, x_ref, o_ref, img_ref):
    wide_rows = x_ref.shape[1] - 2
    patch_len = x_ref.shape[2]
    channels = o_ref.shape[1]
    out_rows = o_ref.shape[2]
    img_ref[...] = jnp.zeros_like(img_ref)
    img_ref[0 : wide_rows + 2, :] = x_ref[0].astype(jnp.float32)
    lane = lax.broadcasted_iota(jnp.int32, (8, patch_len), 1)

    def block(i, carry):
        top = pl.multiple_of(i * 8, 8)
        windows = []
        for tap_row in range(3):
            rows = img_ref[pl.ds(top + tap_row, 8), :]
            left = jnp.where(lane == 0, 0.0, pltpu.roll(rows, 1, 1))
            right = jnp.where(lane == patch_len - 1, 0.0, pltpu.roll(rows, patch_len - 1, 1))
            windows.extend([left, rows, right])
        keep = keep_ref[pl.ds(top, 8), :] > 0
        for c in range(channels):
            acc = jnp.zeros((8, patch_len), jnp.float32) + b_ref[c]
            for t in range(9):
                acc = acc + w_ref[t, c] * windows[t]
            acc = jnp.where(keep, jnp.maximum(acc, 0.0), 0.0)
            o_ref[0, c, pl.ds(top, 8), :] = acc.astype(o_ref.dtype)
        return carry

    lax.fori_loop(0, out_rows // 8, block, 0)


def conv_one(rows_in, inside, conv1_w, conv1_b):
    sec_count, padded_rows, patch_len = rows_in.shape
    wide_rows = padded_rows - 2
    channels = conv1_w.shape[1]
    out_rows = -(-wide_rows // 8) * 8
    keep = jnp.zeros((out_rows, patch_len), jnp.int32).at[:wide_rows].set(
        jnp.broadcast_to(inside.astype(jnp.int32)[:, None], (wide_rows, patch_len))
    )
    return pl.pallas_call(
        conv_one_kernel,
        grid=(sec_count,),
        in_specs=[
            pl.BlockSpec(memory_space=pltpu.SMEM),
            pl.BlockSpec(memory_space=pltpu.SMEM),
            pl.BlockSpec((out_rows, patch_len), lambda s: (0, 0)),
            pl.BlockSpec((1, padded_rows, patch_len), lambda s: (s, 0, 0)),
        ],
        out_specs=pl.BlockSpec((1, channels, out_rows, patch_len), lambda s: (s, 0, 0, 0)),
        out_shape=jax.ShapeDtypeStruct((sec_count, channels, out_rows, patch_len), jnp.bfloat16),
        scratch_shapes=[pltpu.VMEM((out_rows + 8, patch_len), jnp.float32)],
    )(conv1_w.astype(jnp.float32), conv1_b, keep, rows_in)


def conv_layers(rows_in, inside, conv1_w, conv1_b, conv2_w):
    sec_count = rows_in.shape[0]
    wide_rows = rows_in.shape[1] - 2
    strip_rows = wide_rows - 2
    patch_len = rows_in.shape[2]
    channels = conv1_w.shape[1]
    hidden = conv_one(rows_in, inside, conv1_w, conv1_b)
    hidden_pad = jnp.pad(hidden, ((0, 0), (0, 0), (0, 0), (1, 1)))
    layer_two = jnp.zeros((sec_count, channels, strip_rows, patch_len), jnp.float32)
    for tap_row in range(3):
        for tap_col in range(3):
            window = hidden_pad[:, :, tap_row : tap_row + strip_rows, tap_col : tap_col + patch_len]
            layer_two = layer_two + jnp.einsum(
                "schw,co->sohw",
                window,
                conv2_w[3 * tap_row + tap_col],
                preferred_element_type=jnp.float32,
            )
    return layer_two.astype(jnp.bfloat16)


def patch_spectra(features, cosine, sin_table, rows_per):
    sec_count, channels, strip_rows, patch_len = features.shape
    patches = features.reshape(sec_count, channels, rows_per, patch_len, patch_len)
    patches = patches.transpose(0, 2, 1, 3, 4).reshape(-1, patch_len, patch_len)
    flat_rows = patches.reshape(-1, patch_len)
    half_both = jnp.dot(
        flat_rows, jnp.concatenate([cosine, sin_table], axis=1), preferred_element_type=jnp.float32
    ).astype(jnp.bfloat16)
    half_cos = half_both[:, :patch_len].reshape(patches.shape)
    half_sin = half_both[:, patch_len:].reshape(patches.shape)
    left_cos = jnp.concatenate([cosine, -sin_table], axis=0)
    left_sin = jnp.concatenate([-sin_table, -cosine], axis=0)
    spec_both = jnp.einsum(
        "uy,byk->buk", left_cos, half_cos, preferred_element_type=jnp.float32
    ) + jnp.einsum("uy,byk->buk", left_sin, half_sin, preferred_element_type=jnp.float32)
    spec_both = spec_both.astype(jnp.bfloat16)
    spec_real = spec_both[:, :patch_len]
    spec_imag = spec_both[:, patch_len:]
    out_shape = (sec_count, rows_per, channels, patch_len, patch_len)
    return (
        spec_real.reshape(out_shape),
        spec_imag.reshape(out_shape),
    )


def correlate(own_real, own_imag, part_real, part_imag, pair_valid, cosine, sin_table):
    patch_len = own_real.shape[-1]
    channels = own_real.shape[2]
    own_re32 = own_real.astype(jnp.float32)
    own_im32 = own_imag.astype(jnp.float32)
    part_re32 = part_real.astype(jnp.float32)
    part_im32 = part_imag.astype(jnp.float32)
    freq_index = jnp.arange(patch_len, dtype=jnp.int32)
    zero_freq = (freq_index[:, None] == 0) & (freq_index[None, :] == 0)
    cross_real = jnp.sum(own_re32 * part_re32 + own_im32 * part_im32, axis=2).astype(jnp.bfloat16)
    cross_imag = jnp.sum(own_re32 * part_im32 - own_im32 * part_re32, axis=2).astype(jnp.bfloat16)
    drop = zero_freq[None, None] | ~pair_valid[:, None, None, None]
    cross_real = jnp.where(drop, jnp.zeros_like(cross_real), cross_real)
    cross_imag = jnp.where(drop, jnp.zeros_like(cross_imag), cross_imag)
    flat_real = cross_real.reshape(-1, patch_len)
    flat_imag = cross_imag.reshape(-1, patch_len)
    back_both = (
        jnp.dot(
            flat_real,
            jnp.concatenate([cosine, sin_table], axis=1),
            preferred_element_type=jnp.float32,
        )
        + jnp.dot(
            flat_imag,
            jnp.concatenate([-sin_table, cosine], axis=1),
            preferred_element_type=jnp.float32,
        )
    ).astype(jnp.bfloat16)
    back_real = back_both[:, :patch_len]
    back_imag = back_both[:, patch_len:]
    back_real = back_real.reshape(-1, patch_len, patch_len)
    back_imag = back_imag.reshape(-1, patch_len, patch_len)
    raw_corr = jnp.einsum(
        "ju,buk->bjk", cosine, back_real, preferred_element_type=jnp.float32
    ) - jnp.einsum("ju,buk->bjk", sin_table, back_imag, preferred_element_type=jnp.float32)
    scores = raw_corr * (CORR_GAIN / (patch_len * patch_len * patch_len * math.sqrt(channels)))
    flat_scores = scores.reshape(-1, patch_len * patch_len)
    row_max = jnp.max(flat_scores, axis=1, keepdims=True)
    expos = jnp.exp(flat_scores - row_max)
    probability = expos / jnp.sum(expos, axis=1, keepdims=True)
    lag_index = jnp.arange(patch_len, dtype=jnp.int32)
    signed_lag = jnp.where(lag_index >= patch_len // 2, lag_index - patch_len, lag_index).astype(
        jnp.float32
    )
    lag_rows = jnp.broadcast_to(signed_lag[:, None], (patch_len, patch_len)).reshape(-1)
    lag_cols = jnp.broadcast_to(signed_lag[None, :], (patch_len, patch_len)).reshape(-1)
    flow_rows = jnp.sum(probability * lag_rows[None], axis=1) / FLOW_UNIT
    flow_cols = jnp.sum(probability * lag_cols[None], axis=1) / FLOW_UNIT
    return jnp.stack([flow_rows, flow_cols], axis=0)


def local(sections, offsets, valid_mask, conv1_w, conv1_b, conv2_w):
    sec_here = sections.shape[0]
    strip_rows = sections.shape[1]
    patch_len = sections.shape[2]
    rows_per = strip_rows // patch_len
    tile_count = lax.axis_size("tile")
    tile_pos = lax.axis_index("tile")
    cosine, sin_table = dft_tables(patch_len)
    padded_rows = with_halo(sections, (("tile", 1),), 2)
    next_rows = from_behind(padded_rows, "sec", -1)
    row_global = tile_pos * strip_rows - 1 + jnp.arange(strip_rows + 2, dtype=jnp.int32)
    inside = (row_global >= 0) & (row_global < strip_rows * tile_count)
    own_feats = conv_layers(padded_rows, inside, conv1_w, conv1_b, conv2_w)
    own_real, own_imag = patch_spectra(own_feats, cosine, sin_table, rows_per)
    next_feats = conv_layers(next_rows, inside, conv1_w, conv1_b, conv2_w)
    next_real, next_imag = patch_spectra(next_feats, cosine, sin_table, rows_per)
    combined_real = jnp.concatenate([own_real, next_real], axis=0)
    combined_imag = jnp.concatenate([own_imag, next_imag], axis=0)
    use_first = (offsets == 1)[:, None, None, None, None]
    part_real = jnp.where(
        use_first, combined_real[1 : sec_here + 1], combined_real[2 : sec_here + 2]
    )
    part_imag = jnp.where(
        use_first, combined_imag[1 : sec_here + 1], combined_imag[2 : sec_here + 2]
    )
    section_ids = lax.axis_index("sec") * sec_here + jnp.arange(sec_here, dtype=jnp.int32)
    total_sections = sec_here * lax.axis_size("sec")
    pair_valid = section_ids + offsets < total_sections
    flow_est = correlate(
        own_real, own_imag, part_real, part_imag, pair_valid, cosine, sin_table
    ).reshape(2, sec_here, rows_per)
    pair_ok = jnp.where(pair_valid, 1.0, 0.0).astype(jnp.float32)
    weights = valid_mask.astype(jnp.float32) * pair_ok[:, None]
    rows_all = rows_per * tile_count
    grid_y = (
        (tile_pos * rows_per + jnp.arange(rows_per, dtype=jnp.int32)).astype(jnp.float32) + 0.5
    ) / rows_all * 2.0 - 1.0
    weight_y = weights * grid_y[None]
    partial = jnp.concatenate(
        [
            jnp.sum(weights, axis=1)[:, None],
            jnp.sum(weight_y, axis=1)[:, None],
            jnp.sum(weight_y * grid_y[None], axis=1)[:, None],
            jnp.sum(flow_est * weights[None], axis=2).T,
            jnp.sum(flow_est * weight_y[None], axis=2).T,
        ],
        axis=1,
    )
    totals = tile_sum(partial, "tile")
    weight_sum, weighted_y, weighted_yy = totals[:, 0], totals[:, 1], totals[:, 2]
    flow_sum = totals[:, 3:5].T
    flow_y_sum = totals[:, 5:7].T
    m_zero = weight_sum + RIDGE_TERM
    m_two = weighted_yy + RIDGE_TERM
    determinant = m_zero * m_two - weighted_y * weighted_y
    offset_coef = (m_two[None] * flow_sum - weighted_y[None] * flow_y_sum) / determinant[None]
    slope_coef = (m_zero[None] * flow_y_sum - weighted_y[None] * flow_sum) / determinant[None]
    affine = jnp.stack([offset_coef[0], slope_coef[0], offset_coef[1], slope_coef[1]], axis=1)
    fitted = offset_coef[:, :, None] + slope_coef[:, :, None] * grid_y[None, None, :]
    residual = (flow_est - fitted) * weights[None]
    return (residual, affine)


def solution(mesh):
    placed = (P("sec", "tile", None), P("sec"), P("sec", "tile"), P(), P(), P())
    return jax.shard_map(
        local,
        mesh=mesh,
        in_specs=placed,
        out_specs=(P(None, "sec", "tile"), P("sec", None)),
        check_vma=False,
    )
```

```python
import math

import jax
import jax.numpy as jnp
from jax import lax
from jax.sharding import PartitionSpec as P

RIDGE_TERM = 1.0
CORR_GAIN = 2.5
FLOW_UNIT = 8.0


def with_halo(x, sides, width):
    for axis, dim in sides:
        peers, length = (lax.axis_size(axis), x.shape[dim])
        up = [(i, (i + 1) % peers) for i in range(peers - 1)]
        down = [(j, i) for i, j in up]
        last = lax.slice_in_dim(x, length - width, length, axis=dim)
        initial = lax.slice_in_dim(x, 0, width, axis=dim)
        before = lax.ppermute(last, axis, up)
        after = lax.ppermute(initial, axis, down)
        x = jnp.concatenate([before, x, after], axis=dim)
    return x


def from_behind(block, axis, distance):
    devices = range(lax.axis_size(axis))
    route = [(i - distance, i) for i in devices if i - distance in devices]
    return lax.ppermute(block, axis, route)


def tile_sum(v, axis):
    peers = lax.axis_size(axis)
    copies = jnp.broadcast_to(v[None], (peers,) + v.shape)
    return jnp.sum(lax.all_to_all(copies, axis, 0, 0, tiled=False), axis=0)

def dft_tables(patch_len):
    index_row = jnp.arange(patch_len, dtype=jnp.int32)
    product = index_row[:, None] * index_row[None, :] % patch_len
    phase_angle = product.astype(jnp.float32) * (2.0 * math.pi / patch_len)
    return (jnp.cos(phase_angle).astype(jnp.bfloat16), jnp.sin(phase_angle).astype(jnp.bfloat16))


def conv_layers(rows_in, inside, conv1_w, conv1_b, conv2_w):
    sec_count = rows_in.shape[0]
    wide_rows = rows_in.shape[1] - 2
    strip_rows = wide_rows - 2
    patch_len = rows_in.shape[2]
    channels = conv1_w.shape[1]
    padded = jnp.pad(rows_in, ((0, 0), (0, 0), (1, 1)))
    layer_one = (
        jnp.zeros((sec_count, channels, wide_rows, patch_len), jnp.float32)
        + conv1_b[None, :, None, None]
    )
    for tap_row in range(3):
        for tap_col in range(3):
            weight_tap = conv1_w[3 * tap_row + tap_col].astype(jnp.float32)
            window = padded[:, tap_row : tap_row + wide_rows, tap_col : tap_col + patch_len].astype(
                jnp.float32
            )
            layer_one = layer_one + weight_tap[None, :, None, None] * window[:, None]
    hidden = jnp.where(inside[None, None, :, None], jax.nn.relu(layer_one), 0.0).astype(
        jnp.bfloat16
    )
    hidden_pad = jnp.pad(hidden, ((0, 0), (0, 0), (0, 0), (1, 1)))
    layer_two = jnp.zeros((sec_count, channels, strip_rows, patch_len), jnp.float32)
    for tap_row in range(3):
        for tap_col in range(3):
            window = hidden_pad[:, :, tap_row : tap_row + strip_rows, tap_col : tap_col + patch_len]
            layer_two = layer_two + jnp.einsum(
                "schw,co->sohw",
                window,
                conv2_w[3 * tap_row + tap_col],
                preferred_element_type=jnp.float32,
            )
    return layer_two.astype(jnp.bfloat16)


def patch_spectra(features, cosine, sin_table, rows_per):
    sec_count, channels, strip_rows, patch_len = features.shape
    patches = features.reshape(sec_count, channels, rows_per, patch_len, patch_len)
    patches = patches.transpose(0, 2, 1, 3, 4).reshape(-1, patch_len, patch_len)
    flat_rows = patches.reshape(-1, patch_len)
    half_both = jnp.dot(
        flat_rows, jnp.concatenate([cosine, sin_table], axis=1), preferred_element_type=jnp.float32
    ).astype(jnp.bfloat16)
    half_cos = half_both[:, :patch_len].reshape(patches.shape)
    half_sin = half_both[:, patch_len:].reshape(patches.shape)
    left_cos = jnp.concatenate([cosine, -sin_table], axis=0)
    left_sin = jnp.concatenate([-sin_table, -cosine], axis=0)
    spec_both = jnp.einsum(
        "uy,byk->buk", left_cos, half_cos, preferred_element_type=jnp.float32
    ) + jnp.einsum("uy,byk->buk", left_sin, half_sin, preferred_element_type=jnp.float32)
    spec_both = spec_both.astype(jnp.bfloat16)
    spec_real = spec_both[:, :patch_len]
    spec_imag = spec_both[:, patch_len:]
    out_shape = (sec_count, rows_per, channels, patch_len, patch_len)
    return (
        spec_real.reshape(out_shape),
        spec_imag.reshape(out_shape),
    )


def correlate(own_real, own_imag, part_real, part_imag, pair_valid, cosine, sin_table):
    patch_len = own_real.shape[-1]
    channels = own_real.shape[2]
    own_re32 = own_real.astype(jnp.float32)
    own_im32 = own_imag.astype(jnp.float32)
    part_re32 = part_real.astype(jnp.float32)
    part_im32 = part_imag.astype(jnp.float32)
    freq_index = jnp.arange(patch_len, dtype=jnp.int32)
    zero_freq = (freq_index[:, None] == 0) & (freq_index[None, :] == 0)
    cross_real = jnp.sum(own_re32 * part_re32 + own_im32 * part_im32, axis=2).astype(jnp.bfloat16)
    cross_imag = jnp.sum(own_re32 * part_im32 - own_im32 * part_re32, axis=2).astype(jnp.bfloat16)
    drop = zero_freq[None, None] | ~pair_valid[:, None, None, None]
    cross_real = jnp.where(drop, jnp.zeros_like(cross_real), cross_real)
    cross_imag = jnp.where(drop, jnp.zeros_like(cross_imag), cross_imag)
    flat_real = cross_real.reshape(-1, patch_len)
    flat_imag = cross_imag.reshape(-1, patch_len)
    back_both = (
        jnp.dot(
            flat_real,
            jnp.concatenate([cosine, sin_table], axis=1),
            preferred_element_type=jnp.float32,
        )
        + jnp.dot(
            flat_imag,
            jnp.concatenate([-sin_table, cosine], axis=1),
            preferred_element_type=jnp.float32,
        )
    ).astype(jnp.bfloat16)
    back_real = back_both[:, :patch_len]
    back_imag = back_both[:, patch_len:]
    back_real = back_real.reshape(-1, patch_len, patch_len)
    back_imag = back_imag.reshape(-1, patch_len, patch_len)
    raw_corr = jnp.einsum(
        "ju,buk->bjk", cosine, back_real, preferred_element_type=jnp.float32
    ) - jnp.einsum("ju,buk->bjk", sin_table, back_imag, preferred_element_type=jnp.float32)
    scores = raw_corr * (CORR_GAIN / (patch_len * patch_len * patch_len * math.sqrt(channels)))
    flat_scores = scores.reshape(-1, patch_len * patch_len)
    row_max = jnp.max(flat_scores, axis=1, keepdims=True)
    expos = jnp.exp(flat_scores - row_max)
    probability = expos / jnp.sum(expos, axis=1, keepdims=True)
    lag_index = jnp.arange(patch_len, dtype=jnp.int32)
    signed_lag = jnp.where(lag_index >= patch_len // 2, lag_index - patch_len, lag_index).astype(
        jnp.float32
    )
    lag_rows = jnp.broadcast_to(signed_lag[:, None], (patch_len, patch_len)).reshape(-1)
    lag_cols = jnp.broadcast_to(signed_lag[None, :], (patch_len, patch_len)).reshape(-1)
    flow_rows = jnp.sum(probability * lag_rows[None], axis=1) / FLOW_UNIT
    flow_cols = jnp.sum(probability * lag_cols[None], axis=1) / FLOW_UNIT
    return jnp.stack([flow_rows, flow_cols], axis=0)


def local(sections, offsets, valid_mask, conv1_w, conv1_b, conv2_w):
    sec_here = sections.shape[0]
    strip_rows = sections.shape[1]
    patch_len = sections.shape[2]
    rows_per = strip_rows // patch_len
    tile_count = lax.axis_size("tile")
    tile_pos = lax.axis_index("tile")
    cosine, sin_table = dft_tables(patch_len)
    padded_rows = with_halo(sections, (("tile", 1),), 2)
    next_rows = from_behind(padded_rows, "sec", -1)
    row_global = tile_pos * strip_rows - 1 + jnp.arange(strip_rows + 2, dtype=jnp.int32)
    inside = (row_global >= 0) & (row_global < strip_rows * tile_count)
    own_feats = conv_layers(padded_rows, inside, conv1_w, conv1_b, conv2_w)
    own_real, own_imag = patch_spectra(own_feats, cosine, sin_table, rows_per)
    next_feats = conv_layers(next_rows, inside, conv1_w, conv1_b, conv2_w)
    next_real, next_imag = patch_spectra(next_feats, cosine, sin_table, rows_per)
    combined_real = jnp.concatenate([own_real, next_real], axis=0)
    combined_imag = jnp.concatenate([own_imag, next_imag], axis=0)
    use_first = (offsets == 1)[:, None, None, None, None]
    part_real = jnp.where(
        use_first, combined_real[1 : sec_here + 1], combined_real[2 : sec_here + 2]
    )
    part_imag = jnp.where(
        use_first, combined_imag[1 : sec_here + 1], combined_imag[2 : sec_here + 2]
    )
    section_ids = lax.axis_index("sec") * sec_here + jnp.arange(sec_here, dtype=jnp.int32)
    total_sections = sec_here * lax.axis_size("sec")
    pair_valid = section_ids + offsets < total_sections
    flow_est = correlate(
        own_real, own_imag, part_real, part_imag, pair_valid, cosine, sin_table
    ).reshape(2, sec_here, rows_per)
    pair_ok = jnp.where(pair_valid, 1.0, 0.0).astype(jnp.float32)
    weights = valid_mask.astype(jnp.float32) * pair_ok[:, None]
    rows_all = rows_per * tile_count
    grid_y = (
        (tile_pos * rows_per + jnp.arange(rows_per, dtype=jnp.int32)).astype(jnp.float32) + 0.5
    ) / rows_all * 2.0 - 1.0
    weight_y = weights * grid_y[None]
    partial = jnp.concatenate(
        [
            jnp.sum(weights, axis=1)[:, None],
            jnp.sum(weight_y, axis=1)[:, None],
            jnp.sum(weight_y * grid_y[None], axis=1)[:, None],
            jnp.sum(flow_est * weights[None], axis=2).T,
            jnp.sum(flow_est * weight_y[None], axis=2).T,
        ],
        axis=1,
    )
    totals = tile_sum(partial, "tile")
    weighted_y = totals[:, 1:2]
    m_zero = totals[:, 0:1] + RIDGE_TERM
    m_two = totals[:, 2:3] + RIDGE_TERM
    determinant = m_zero * m_two - weighted_y * weighted_y
    flow_sum = totals[:, 3:5]
    flow_y_sum = totals[:, 5:7]
    offset_coef = (m_two * flow_sum - weighted_y * flow_y_sum) / determinant
    slope_coef = (m_zero * flow_y_sum - weighted_y * flow_sum) / determinant
    affine = jnp.stack([offset_coef, slope_coef], axis=2).reshape(sec_here, 4)
    fitted = offset_coef.T[:, :, None] + slope_coef.T[:, :, None] * grid_y[None, None, :]
    residual = (flow_est - fitted) * weights[None]
    return (residual, affine)


def solution(mesh):
    placed = (P("sec", "tile", None), P("sec"), P("sec", "tile"), P(), P(), P())
    return jax.shard_map(
        local,
        mesh=mesh,
        in_specs=placed,
        out_specs=(P(None, "sec", "tile"), P("sec", None)),
        check_vma=False,
    )
```

```python
import math

import jax
import jax.numpy as jnp
from jax import lax
from jax.sharding import PartitionSpec as P

RIDGE_TERM = 1.0
CORR_GAIN = 2.5
FLOW_UNIT = 8.0


def with_halo(x, sides, width):
    for axis, dim in sides:
        peers, length = (lax.axis_size(axis), x.shape[dim])
        up = [(i, (i + 1) % peers) for i in range(peers - 1)]
        down = [(j, i) for i, j in up]
        last = lax.slice_in_dim(x, length - width, length, axis=dim)
        initial = lax.slice_in_dim(x, 0, width, axis=dim)
        before = lax.ppermute(last, axis, up)
        after = lax.ppermute(initial, axis, down)
        x = jnp.concatenate([before, x, after], axis=dim)
    return x


def from_behind(block, axis, distance):
    devices = range(lax.axis_size(axis))
    route = [(i - distance, i) for i in devices if i - distance in devices]
    return lax.ppermute(block, axis, route)


def tile_sum(v, axis):
    peers = lax.axis_size(axis)
    copies = jnp.broadcast_to(v[None], (peers,) + v.shape)
    return jnp.sum(lax.all_to_all(copies, axis, 0, 0, tiled=False), axis=0)

def dft_tables(patch_len):
    index_row = jnp.arange(patch_len, dtype=jnp.int32)
    product = index_row[:, None] * index_row[None, :] % patch_len
    phase_angle = product.astype(jnp.float32) * (2.0 * math.pi / patch_len)
    return (jnp.cos(phase_angle).astype(jnp.bfloat16), jnp.sin(phase_angle).astype(jnp.bfloat16))


def conv_layers(rows_in, inside, conv1_w, conv1_b, conv2_w):
    sec_count = rows_in.shape[0]
    wide_rows = rows_in.shape[1] - 2
    strip_rows = wide_rows - 2
    patch_len = rows_in.shape[2]
    channels = conv1_w.shape[1]
    padded = jnp.pad(rows_in, ((0, 0), (0, 0), (1, 1)))
    layer_one = (
        jnp.zeros((sec_count, channels, wide_rows, patch_len), jnp.float32)
        + conv1_b[None, :, None, None]
    )
    for tap_row in range(3):
        for tap_col in range(3):
            weight_tap = conv1_w[3 * tap_row + tap_col].astype(jnp.float32)
            window = padded[:, tap_row : tap_row + wide_rows, tap_col : tap_col + patch_len].astype(
                jnp.float32
            )
            layer_one = layer_one + weight_tap[None, :, None, None] * window[:, None]
    hidden = jnp.where(inside[None, None, :, None], jax.nn.relu(layer_one), 0.0).astype(
        jnp.bfloat16
    )
    hidden_pad = jnp.pad(hidden, ((0, 0), (0, 0), (0, 0), (1, 1)))
    layer_two = jnp.zeros((sec_count, channels, strip_rows, patch_len), jnp.float32)
    for tap_row in range(3):
        for tap_col in range(3):
            window = hidden_pad[:, :, tap_row : tap_row + strip_rows, tap_col : tap_col + patch_len]
            layer_two = layer_two + jnp.einsum(
                "schw,co->sohw",
                window,
                conv2_w[3 * tap_row + tap_col],
                preferred_element_type=jnp.float32,
            )
    return layer_two.astype(jnp.bfloat16)


def patch_spectra(features, cosine, sin_table, rows_per):
    sec_count, channels, strip_rows, patch_len = features.shape
    patches = features.reshape(sec_count, channels, rows_per, patch_len, patch_len)
    patches = patches.transpose(0, 2, 1, 3, 4).reshape(-1, patch_len, patch_len)
    flat_rows = patches.reshape(-1, patch_len)
    half_both = jnp.dot(
        flat_rows, jnp.concatenate([cosine, sin_table], axis=1), preferred_element_type=jnp.float32
    ).astype(jnp.bfloat16)
    half_cos = half_both[:, :patch_len].reshape(patches.shape)
    half_sin = half_both[:, patch_len:].reshape(patches.shape)
    left_cos = jnp.concatenate([cosine, -sin_table], axis=0)
    left_sin = jnp.concatenate([-sin_table, -cosine], axis=0)
    spec_both = jnp.einsum(
        "uy,byk->buk", left_cos, half_cos, preferred_element_type=jnp.float32
    ) + jnp.einsum("uy,byk->buk", left_sin, half_sin, preferred_element_type=jnp.float32)
    spec_both = spec_both.astype(jnp.bfloat16)
    return spec_both.reshape(sec_count, rows_per, channels, 2 * patch_len, patch_len)


def correlate(own_real, own_imag, part_real, part_imag, pair_valid, cosine, sin_table):
    patch_len = own_real.shape[-1]
    channels = own_real.shape[2]
    own_re32 = own_real.astype(jnp.float32)
    own_im32 = own_imag.astype(jnp.float32)
    part_re32 = part_real.astype(jnp.float32)
    part_im32 = part_imag.astype(jnp.float32)
    freq_index = jnp.arange(patch_len, dtype=jnp.int32)
    zero_freq = (freq_index[:, None] == 0) & (freq_index[None, :] == 0)
    cross_real = jnp.sum(own_re32 * part_re32 + own_im32 * part_im32, axis=2).astype(jnp.bfloat16)
    cross_imag = jnp.sum(own_re32 * part_im32 - own_im32 * part_re32, axis=2).astype(jnp.bfloat16)
    drop = zero_freq[None, None] | ~pair_valid[:, None, None, None]
    cross_real = jnp.where(drop, jnp.zeros_like(cross_real), cross_real)
    cross_imag = jnp.where(drop, jnp.zeros_like(cross_imag), cross_imag)
    flat_real = cross_real.reshape(-1, patch_len)
    flat_imag = cross_imag.reshape(-1, patch_len)
    back_both = (
        jnp.dot(
            flat_real,
            jnp.concatenate([cosine, sin_table], axis=1),
            preferred_element_type=jnp.float32,
        )
        + jnp.dot(
            flat_imag,
            jnp.concatenate([-sin_table, cosine], axis=1),
            preferred_element_type=jnp.float32,
        )
    ).astype(jnp.bfloat16)
    back_real = back_both[:, :patch_len]
    back_imag = back_both[:, patch_len:]
    back_real = back_real.reshape(-1, patch_len, patch_len)
    back_imag = back_imag.reshape(-1, patch_len, patch_len)
    raw_corr = jnp.einsum(
        "ju,buk->bjk", cosine, back_real, preferred_element_type=jnp.float32
    ) - jnp.einsum("ju,buk->bjk", sin_table, back_imag, preferred_element_type=jnp.float32)
    scores = raw_corr * (CORR_GAIN / (patch_len * patch_len * patch_len * math.sqrt(channels)))
    flat_scores = scores.reshape(-1, patch_len * patch_len)
    row_max = jnp.max(flat_scores, axis=1, keepdims=True)
    expos = jnp.exp(flat_scores - row_max)
    probability = expos / jnp.sum(expos, axis=1, keepdims=True)
    lag_index = jnp.arange(patch_len, dtype=jnp.int32)
    signed_lag = jnp.where(lag_index >= patch_len // 2, lag_index - patch_len, lag_index).astype(
        jnp.float32
    )
    lag_rows = jnp.broadcast_to(signed_lag[:, None], (patch_len, patch_len)).reshape(-1)
    lag_cols = jnp.broadcast_to(signed_lag[None, :], (patch_len, patch_len)).reshape(-1)
    flow_rows = jnp.sum(probability * lag_rows[None], axis=1) / FLOW_UNIT
    flow_cols = jnp.sum(probability * lag_cols[None], axis=1) / FLOW_UNIT
    return jnp.stack([flow_rows, flow_cols], axis=0)


def local(sections, offsets, valid_mask, conv1_w, conv1_b, conv2_w):
    sec_here = sections.shape[0]
    strip_rows = sections.shape[1]
    patch_len = sections.shape[2]
    rows_per = strip_rows // patch_len
    tile_count = lax.axis_size("tile")
    tile_pos = lax.axis_index("tile")
    cosine, sin_table = dft_tables(patch_len)
    padded_rows = with_halo(sections, (("tile", 1),), 2)
    next_rows = from_behind(padded_rows, "sec", -1)
    row_global = tile_pos * strip_rows - 1 + jnp.arange(strip_rows + 2, dtype=jnp.int32)
    inside = (row_global >= 0) & (row_global < strip_rows * tile_count)
    own_feats = conv_layers(padded_rows, inside, conv1_w, conv1_b, conv2_w)
    own_both = patch_spectra(own_feats, cosine, sin_table, rows_per)
    next_feats = conv_layers(next_rows, inside, conv1_w, conv1_b, conv2_w)
    next_both = patch_spectra(next_feats, cosine, sin_table, rows_per)
    combined = jnp.concatenate([own_both, next_both], axis=0)
    use_first = (offsets == 1)[:, None, None, None, None]
    part_both = jnp.where(use_first, combined[1 : sec_here + 1], combined[2 : sec_here + 2])
    own_real, own_imag = own_both[..., :patch_len, :], own_both[..., patch_len:, :]
    part_real, part_imag = part_both[..., :patch_len, :], part_both[..., patch_len:, :]
    section_ids = lax.axis_index("sec") * sec_here + jnp.arange(sec_here, dtype=jnp.int32)
    total_sections = sec_here * lax.axis_size("sec")
    pair_valid = section_ids + offsets < total_sections
    flow_est = correlate(
        own_real, own_imag, part_real, part_imag, pair_valid, cosine, sin_table
    ).reshape(2, sec_here, rows_per)
    pair_ok = jnp.where(pair_valid, 1.0, 0.0).astype(jnp.float32)
    weights = valid_mask.astype(jnp.float32) * pair_ok[:, None]
    rows_all = rows_per * tile_count
    grid_y = (
        (tile_pos * rows_per + jnp.arange(rows_per, dtype=jnp.int32)).astype(jnp.float32) + 0.5
    ) / rows_all * 2.0 - 1.0
    weight_y = weights * grid_y[None]
    partial = jnp.concatenate(
        [
            jnp.sum(weights, axis=1)[:, None],
            jnp.sum(weight_y, axis=1)[:, None],
            jnp.sum(weight_y * grid_y[None], axis=1)[:, None],
            jnp.sum(flow_est * weights[None], axis=2).T,
            jnp.sum(flow_est * weight_y[None], axis=2).T,
        ],
        axis=1,
    )
    totals = tile_sum(partial, "tile")
    weight_sum, weighted_y, weighted_yy = totals[:, 0], totals[:, 1], totals[:, 2]
    flow_sum = totals[:, 3:5].T
    flow_y_sum = totals[:, 5:7].T
    m_zero = weight_sum + RIDGE_TERM
    m_two = weighted_yy + RIDGE_TERM
    determinant = m_zero * m_two - weighted_y * weighted_y
    offset_coef = (m_two[None] * flow_sum - weighted_y[None] * flow_y_sum) / determinant[None]
    slope_coef = (m_zero[None] * flow_y_sum - weighted_y[None] * flow_sum) / determinant[None]
    affine = jnp.stack([offset_coef[0], slope_coef[0], offset_coef[1], slope_coef[1]], axis=1)
    fitted = offset_coef[:, :, None] + slope_coef[:, :, None] * grid_y[None, None, :]
    residual = (flow_est - fitted) * weights[None]
    return (residual, affine)


def solution(mesh):
    placed = (P("sec", "tile", None), P("sec"), P("sec", "tile"), P(), P(), P())
    return jax.shard_map(
        local,
        mesh=mesh,
        in_specs=placed,
        out_specs=(P(None, "sec", "tile"), P("sec", None)),
        check_vma=False,
    )
```

```python
import math

import jax
import jax.numpy as jnp
from jax import lax
from jax.sharding import PartitionSpec as P

RIDGE_TERM = 1.0
CORR_GAIN = 2.5
FLOW_UNIT = 8.0


def with_halo(x, sides, width):
    for axis, dim in sides:
        peers, length = (lax.axis_size(axis), x.shape[dim])
        up = [(i, (i + 1) % peers) for i in range(peers - 1)]
        down = [(j, i) for i, j in up]
        last = lax.slice_in_dim(x, length - width, length, axis=dim)
        initial = lax.slice_in_dim(x, 0, width, axis=dim)
        before = lax.ppermute(last, axis, up)
        after = lax.ppermute(initial, axis, down)
        x = jnp.concatenate([before, x, after], axis=dim)
    return x


def from_behind(block, axis, distance):
    devices = range(lax.axis_size(axis))
    route = [(i - distance, i) for i in devices if i - distance in devices]
    return lax.ppermute(block, axis, route)


def tile_sum(v, axis):
    peers = lax.axis_size(axis)
    copies = jnp.broadcast_to(v[None], (peers,) + v.shape)
    return jnp.sum(lax.all_to_all(copies, axis, 0, 0, tiled=False), axis=0)

def dft_tables(patch_len):
    index_row = jnp.arange(patch_len, dtype=jnp.int32)
    product = index_row[:, None] * index_row[None, :] % patch_len
    phase_angle = product.astype(jnp.float32) * (2.0 * math.pi / patch_len)
    return (jnp.cos(phase_angle).astype(jnp.bfloat16), jnp.sin(phase_angle).astype(jnp.bfloat16))


def conv_layers(rows_in, inside, conv1_w, conv1_b, conv2_w):
    sec_count = rows_in.shape[0]
    wide_rows = rows_in.shape[1] - 2
    strip_rows = wide_rows - 2
    patch_len = rows_in.shape[2]
    channels = conv1_w.shape[1]
    padded = jnp.pad(rows_in.astype(jnp.float32), ((0, 0), (0, 0), (1, 1)))
    layer_one = (
        jnp.zeros((sec_count, channels, wide_rows, patch_len), jnp.float32)
        + conv1_b[None, :, None, None]
    )
    for tap_row in range(3):
        for tap_col in range(3):
            weight_tap = conv1_w[3 * tap_row + tap_col].astype(jnp.float32)
            window = padded[:, tap_row : tap_row + wide_rows, tap_col : tap_col + patch_len]
            layer_one = layer_one + weight_tap[None, :, None, None] * window[:, None]
    hidden = jnp.where(inside[None, None, :, None], jax.nn.relu(layer_one), 0.0).astype(
        jnp.bfloat16
    )
    hidden_pad = jnp.pad(hidden, ((0, 0), (0, 0), (0, 0), (1, 1)))
    layer_two = jnp.zeros((sec_count, channels, strip_rows, patch_len), jnp.float32)
    for tap_row in range(3):
        for tap_col in range(3):
            window = hidden_pad[:, :, tap_row : tap_row + strip_rows, tap_col : tap_col + patch_len]
            layer_two = layer_two + jnp.einsum(
                "schw,co->sohw",
                window,
                conv2_w[3 * tap_row + tap_col],
                preferred_element_type=jnp.float32,
            )
    return layer_two.astype(jnp.bfloat16)


def patch_spectra(features, cosine, sin_table, rows_per):
    sec_count, channels, strip_rows, patch_len = features.shape
    patches = features.reshape(sec_count, channels, rows_per, patch_len, patch_len)
    patches = patches.transpose(0, 2, 1, 3, 4).reshape(-1, patch_len, patch_len)
    flat_rows = patches.reshape(-1, patch_len)
    half_both = jnp.dot(
        flat_rows, jnp.concatenate([cosine, sin_table], axis=1), preferred_element_type=jnp.float32
    ).astype(jnp.bfloat16)
    half_cos = half_both[:, :patch_len].reshape(patches.shape)
    half_sin = half_both[:, patch_len:].reshape(patches.shape)
    left_cos = jnp.concatenate([cosine, -sin_table], axis=0)
    left_sin = jnp.concatenate([-sin_table, -cosine], axis=0)
    spec_both = jnp.einsum(
        "uy,byk->buk", left_cos, half_cos, preferred_element_type=jnp.float32
    ) + jnp.einsum("uy,byk->buk", left_sin, half_sin, preferred_element_type=jnp.float32)
    spec_both = spec_both.astype(jnp.bfloat16)
    spec_real = spec_both[:, :patch_len]
    spec_imag = spec_both[:, patch_len:]
    out_shape = (sec_count, rows_per, channels, patch_len, patch_len)
    return (
        spec_real.reshape(out_shape),
        spec_imag.reshape(out_shape),
    )


def correlate(own_real, own_imag, part_real, part_imag, pair_valid, cosine, sin_table):
    patch_len = own_real.shape[-1]
    channels = own_real.shape[2]
    own_re32 = own_real.astype(jnp.float32)
    own_im32 = own_imag.astype(jnp.float32)
    part_re32 = part_real.astype(jnp.float32)
    part_im32 = part_imag.astype(jnp.float32)
    freq_index = jnp.arange(patch_len, dtype=jnp.int32)
    zero_freq = (freq_index[:, None] == 0) & (freq_index[None, :] == 0)
    cross_real = jnp.sum(own_re32 * part_re32 + own_im32 * part_im32, axis=2).astype(jnp.bfloat16)
    cross_imag = jnp.sum(own_re32 * part_im32 - own_im32 * part_re32, axis=2).astype(jnp.bfloat16)
    drop = zero_freq[None, None] | ~pair_valid[:, None, None, None]
    cross_real = jnp.where(drop, jnp.zeros_like(cross_real), cross_real)
    cross_imag = jnp.where(drop, jnp.zeros_like(cross_imag), cross_imag)
    flat_real = cross_real.reshape(-1, patch_len)
    flat_imag = cross_imag.reshape(-1, patch_len)
    back_both = (
        jnp.dot(
            flat_real,
            jnp.concatenate([cosine, sin_table], axis=1),
            preferred_element_type=jnp.float32,
        )
        + jnp.dot(
            flat_imag,
            jnp.concatenate([-sin_table, cosine], axis=1),
            preferred_element_type=jnp.float32,
        )
    ).astype(jnp.bfloat16)
    back_real = back_both[:, :patch_len]
    back_imag = back_both[:, patch_len:]
    back_real = back_real.reshape(-1, patch_len, patch_len)
    back_imag = back_imag.reshape(-1, patch_len, patch_len)
    raw_corr = jnp.einsum(
        "ju,buk->bjk", cosine, back_real, preferred_element_type=jnp.float32
    ) - jnp.einsum("ju,buk->bjk", sin_table, back_imag, preferred_element_type=jnp.float32)
    scores = raw_corr * (CORR_GAIN / (patch_len * patch_len * patch_len * math.sqrt(channels)))
    flat_scores = scores.reshape(-1, patch_len * patch_len)
    row_max = jnp.max(flat_scores, axis=1, keepdims=True)
    expos = jnp.exp(flat_scores - row_max)
    probability = expos / jnp.sum(expos, axis=1, keepdims=True)
    lag_index = jnp.arange(patch_len, dtype=jnp.int32)
    signed_lag = jnp.where(lag_index >= patch_len // 2, lag_index - patch_len, lag_index).astype(
        jnp.float32
    )
    lag_rows = jnp.broadcast_to(signed_lag[:, None], (patch_len, patch_len)).reshape(-1)
    lag_cols = jnp.broadcast_to(signed_lag[None, :], (patch_len, patch_len)).reshape(-1)
    flow_rows = jnp.sum(probability * lag_rows[None], axis=1) / FLOW_UNIT
    flow_cols = jnp.sum(probability * lag_cols[None], axis=1) / FLOW_UNIT
    return jnp.stack([flow_rows, flow_cols], axis=0)


def local(sections, offsets, valid_mask, conv1_w, conv1_b, conv2_w):
    sec_here = sections.shape[0]
    strip_rows = sections.shape[1]
    patch_len = sections.shape[2]
    rows_per = strip_rows // patch_len
    tile_count = lax.axis_size("tile")
    tile_pos = lax.axis_index("tile")
    cosine, sin_table = dft_tables(patch_len)
    padded_rows = with_halo(sections, (("tile", 1),), 2)
    next_rows = from_behind(padded_rows, "sec", -1)
    row_global = tile_pos * strip_rows - 1 + jnp.arange(strip_rows + 2, dtype=jnp.int32)
    inside = (row_global >= 0) & (row_global < strip_rows * tile_count)
    own_feats = conv_layers(padded_rows, inside, conv1_w, conv1_b, conv2_w)
    own_real, own_imag = patch_spectra(own_feats, cosine, sin_table, rows_per)
    next_feats = conv_layers(next_rows, inside, conv1_w, conv1_b, conv2_w)
    next_real, next_imag = patch_spectra(next_feats, cosine, sin_table, rows_per)
    combined_real = jnp.concatenate([own_real, next_real], axis=0)
    combined_imag = jnp.concatenate([own_imag, next_imag], axis=0)
    use_first = (offsets == 1)[:, None, None, None, None]
    part_real = jnp.where(
        use_first, combined_real[1 : sec_here + 1], combined_real[2 : sec_here + 2]
    )
    part_imag = jnp.where(
        use_first, combined_imag[1 : sec_here + 1], combined_imag[2 : sec_here + 2]
    )
    section_ids = lax.axis_index("sec") * sec_here + jnp.arange(sec_here, dtype=jnp.int32)
    total_sections = sec_here * lax.axis_size("sec")
    pair_valid = section_ids + offsets < total_sections
    flow_est = correlate(
        own_real, own_imag, part_real, part_imag, pair_valid, cosine, sin_table
    ).reshape(2, sec_here, rows_per)
    pair_ok = jnp.where(pair_valid, 1.0, 0.0).astype(jnp.float32)
    weights = valid_mask.astype(jnp.float32) * pair_ok[:, None]
    rows_all = rows_per * tile_count
    grid_y = (
        (tile_pos * rows_per + jnp.arange(rows_per, dtype=jnp.int32)).astype(jnp.float32) + 0.5
    ) / rows_all * 2.0 - 1.0
    weight_y = weights * grid_y[None]
    partial = jnp.concatenate(
        [
            jnp.sum(weights, axis=1)[:, None],
            jnp.sum(weight_y, axis=1)[:, None],
            jnp.sum(weight_y * grid_y[None], axis=1)[:, None],
            jnp.sum(flow_est * weights[None], axis=2).T,
            jnp.sum(flow_est * weight_y[None], axis=2).T,
        ],
        axis=1,
    )
    totals = tile_sum(partial, "tile")
    weight_sum, weighted_y, weighted_yy = totals[:, 0], totals[:, 1], totals[:, 2]
    flow_sum = totals[:, 3:5].T
    flow_y_sum = totals[:, 5:7].T
    m_zero = weight_sum + RIDGE_TERM
    m_two = weighted_yy + RIDGE_TERM
    determinant = m_zero * m_two - weighted_y * weighted_y
    offset_coef = (m_two[None] * flow_sum - weighted_y[None] * flow_y_sum) / determinant[None]
    slope_coef = (m_zero[None] * flow_y_sum - weighted_y[None] * flow_sum) / determinant[None]
    affine = jnp.stack([offset_coef[0], slope_coef[0], offset_coef[1], slope_coef[1]], axis=1)
    fitted = offset_coef[:, :, None] + slope_coef[:, :, None] * grid_y[None, None, :]
    residual = (flow_est - fitted) * weights[None]
    return (residual, affine)


def solution(mesh):
    placed = (P("sec", "tile", None), P("sec"), P("sec", "tile"), P(), P(), P())
    return jax.shard_map(
        local,
        mesh=mesh,
        in_specs=placed,
        out_specs=(P(None, "sec", "tile"), P("sec", None)),
        check_vma=False,
    )
```

```python
import math

import jax
import jax.numpy as jnp
from jax import lax
from jax.sharding import PartitionSpec as P

RIDGE_TERM = 1.0
CORR_GAIN = 2.5
FLOW_UNIT = 8.0


def with_halo(x, sides, width):
    for axis, dim in sides:
        peers, length = (lax.axis_size(axis), x.shape[dim])
        up = [(i, (i + 1) % peers) for i in range(peers - 1)]
        down = [(j, i) for i, j in up]
        last = lax.slice_in_dim(x, length - width, length, axis=dim)
        initial = lax.slice_in_dim(x, 0, width, axis=dim)
        before = lax.ppermute(last, axis, up)
        after = lax.ppermute(initial, axis, down)
        x = jnp.concatenate([before, x, after], axis=dim)
    return x


def from_behind(block, axis, distance):
    devices = range(lax.axis_size(axis))
    route = [(i - distance, i) for i in devices if i - distance in devices]
    return lax.ppermute(block, axis, route)


def tile_sum(v, axis):
    peers = lax.axis_size(axis)
    copies = jnp.broadcast_to(v[None], (peers,) + v.shape)
    return jnp.sum(lax.all_to_all(copies, axis, 0, 0, tiled=False), axis=0)

def dft_tables(patch_len):
    index_row = jnp.arange(patch_len, dtype=jnp.int32)
    product = index_row[:, None] * index_row[None, :] % patch_len
    phase_angle = product.astype(jnp.float32) * (2.0 * math.pi / patch_len)
    return (jnp.cos(phase_angle).astype(jnp.bfloat16), jnp.sin(phase_angle).astype(jnp.bfloat16))


def conv_layers(rows_in, inside, conv1_w, conv1_b, conv2_w):
    sec_count = rows_in.shape[0]
    wide_rows = rows_in.shape[1] - 2
    strip_rows = wide_rows - 2
    patch_len = rows_in.shape[2]
    channels = conv1_w.shape[1]
    padded = jnp.pad(rows_in, ((0, 0), (0, 0), (1, 1)))
    layer_one = (
        jnp.zeros((sec_count, channels, wide_rows, patch_len), jnp.float32)
        + conv1_b[None, :, None, None]
    )
    for tap_row in range(3):
        for tap_col in range(3):
            weight_tap = conv1_w[3 * tap_row + tap_col].astype(jnp.float32)
            window = padded[:, tap_row : tap_row + wide_rows, tap_col : tap_col + patch_len].astype(
                jnp.float32
            )
            layer_one = layer_one + weight_tap[None, :, None, None] * window[:, None]
    hidden = jnp.where(inside[None, None, :, None], jax.nn.relu(layer_one), 0.0).astype(
        jnp.bfloat16
    )
    hidden_pad = jnp.pad(hidden, ((0, 0), (0, 0), (0, 0), (1, 1)))
    layer_two = None
    for tap_row in range(3):
        for tap_col in range(3):
            window = hidden_pad[:, :, tap_row : tap_row + strip_rows, tap_col : tap_col + patch_len]
            term = jnp.einsum(
                "schw,co->sohw",
                window,
                conv2_w[3 * tap_row + tap_col],
                preferred_element_type=jnp.float32,
            )
            layer_two = term if layer_two is None else layer_two + term
    return layer_two.astype(jnp.bfloat16)


def patch_spectra(features, cosine, sin_table, rows_per):
    sec_count, channels, strip_rows, patch_len = features.shape
    patches = features.reshape(sec_count, channels, rows_per, patch_len, patch_len)
    patches = patches.transpose(0, 2, 1, 3, 4).reshape(-1, patch_len, patch_len)
    flat_rows = patches.reshape(-1, patch_len)
    half_both = jnp.dot(
        flat_rows, jnp.concatenate([cosine, sin_table], axis=1), preferred_element_type=jnp.float32
    ).astype(jnp.bfloat16)
    half_cos = half_both[:, :patch_len].reshape(patches.shape)
    half_sin = half_both[:, patch_len:].reshape(patches.shape)
    left_cos = jnp.concatenate([cosine, -sin_table], axis=0)
    left_sin = jnp.concatenate([-sin_table, -cosine], axis=0)
    spec_both = jnp.einsum(
        "uy,byk->buk", left_cos, half_cos, preferred_element_type=jnp.float32
    ) + jnp.einsum("uy,byk->buk", left_sin, half_sin, preferred_element_type=jnp.float32)
    spec_both = spec_both.astype(jnp.bfloat16)
    spec_real = spec_both[:, :patch_len]
    spec_imag = spec_both[:, patch_len:]
    out_shape = (sec_count, rows_per, channels, patch_len, patch_len)
    return (
        spec_real.reshape(out_shape),
        spec_imag.reshape(out_shape),
    )


def correlate(own_real, own_imag, part_real, part_imag, pair_valid, cosine, sin_table):
    patch_len = own_real.shape[-1]
    channels = own_real.shape[2]
    own_re32 = own_real.astype(jnp.float32)
    own_im32 = own_imag.astype(jnp.float32)
    part_re32 = part_real.astype(jnp.float32)
    part_im32 = part_imag.astype(jnp.float32)
    freq_index = jnp.arange(patch_len, dtype=jnp.int32)
    zero_freq = (freq_index[:, None] == 0) & (freq_index[None, :] == 0)
    cross_real = jnp.sum(own_re32 * part_re32 + own_im32 * part_im32, axis=2).astype(jnp.bfloat16)
    cross_imag = jnp.sum(own_re32 * part_im32 - own_im32 * part_re32, axis=2).astype(jnp.bfloat16)
    drop = zero_freq[None, None] | ~pair_valid[:, None, None, None]
    cross_real = jnp.where(drop, jnp.zeros_like(cross_real), cross_real)
    cross_imag = jnp.where(drop, jnp.zeros_like(cross_imag), cross_imag)
    flat_real = cross_real.reshape(-1, patch_len)
    flat_imag = cross_imag.reshape(-1, patch_len)
    back_both = (
        jnp.dot(
            flat_real,
            jnp.concatenate([cosine, sin_table], axis=1),
            preferred_element_type=jnp.float32,
        )
        + jnp.dot(
            flat_imag,
            jnp.concatenate([-sin_table, cosine], axis=1),
            preferred_element_type=jnp.float32,
        )
    ).astype(jnp.bfloat16)
    back_real = back_both[:, :patch_len]
    back_imag = back_both[:, patch_len:]
    back_real = back_real.reshape(-1, patch_len, patch_len)
    back_imag = back_imag.reshape(-1, patch_len, patch_len)
    raw_corr = jnp.einsum(
        "ju,buk->bjk", cosine, back_real, preferred_element_type=jnp.float32
    ) - jnp.einsum("ju,buk->bjk", sin_table, back_imag, preferred_element_type=jnp.float32)
    scores = raw_corr * (CORR_GAIN / (patch_len * patch_len * patch_len * math.sqrt(channels)))
    flat_scores = scores.reshape(-1, patch_len * patch_len)
    row_max = jnp.max(flat_scores, axis=1, keepdims=True)
    expos = jnp.exp(flat_scores - row_max)
    probability = expos / jnp.sum(expos, axis=1, keepdims=True)
    lag_index = jnp.arange(patch_len, dtype=jnp.int32)
    signed_lag = jnp.where(lag_index >= patch_len // 2, lag_index - patch_len, lag_index).astype(
        jnp.float32
    )
    lag_rows = jnp.broadcast_to(signed_lag[:, None], (patch_len, patch_len)).reshape(-1)
    lag_cols = jnp.broadcast_to(signed_lag[None, :], (patch_len, patch_len)).reshape(-1)
    flow_rows = jnp.sum(probability * lag_rows[None], axis=1) / FLOW_UNIT
    flow_cols = jnp.sum(probability * lag_cols[None], axis=1) / FLOW_UNIT
    return jnp.stack([flow_rows, flow_cols], axis=0)


def local(sections, offsets, valid_mask, conv1_w, conv1_b, conv2_w):
    sec_here = sections.shape[0]
    strip_rows = sections.shape[1]
    patch_len = sections.shape[2]
    rows_per = strip_rows // patch_len
    tile_count = lax.axis_size("tile")
    tile_pos = lax.axis_index("tile")
    cosine, sin_table = dft_tables(patch_len)
    padded_rows = with_halo(sections, (("tile", 1),), 2)
    next_rows = from_behind(padded_rows, "sec", -1)
    row_global = tile_pos * strip_rows - 1 + jnp.arange(strip_rows + 2, dtype=jnp.int32)
    inside = (row_global >= 0) & (row_global < strip_rows * tile_count)
    own_feats = conv_layers(padded_rows, inside, conv1_w, conv1_b, conv2_w)
    own_real, own_imag = patch_spectra(own_feats, cosine, sin_table, rows_per)
    next_feats = conv_layers(next_rows, inside, conv1_w, conv1_b, conv2_w)
    next_real, next_imag = patch_spectra(next_feats, cosine, sin_table, rows_per)
    combined_real = jnp.concatenate([own_real, next_real], axis=0)
    combined_imag = jnp.concatenate([own_imag, next_imag], axis=0)
    use_first = (offsets == 1)[:, None, None, None, None]
    part_real = jnp.where(
        use_first, combined_real[1 : sec_here + 1], combined_real[2 : sec_here + 2]
    )
    part_imag = jnp.where(
        use_first, combined_imag[1 : sec_here + 1], combined_imag[2 : sec_here + 2]
    )
    section_ids = lax.axis_index("sec") * sec_here + jnp.arange(sec_here, dtype=jnp.int32)
    total_sections = sec_here * lax.axis_size("sec")
    pair_valid = section_ids + offsets < total_sections
    flow_est = correlate(
        own_real, own_imag, part_real, part_imag, pair_valid, cosine, sin_table
    ).reshape(2, sec_here, rows_per)
    pair_ok = jnp.where(pair_valid, 1.0, 0.0).astype(jnp.float32)
    weights = valid_mask.astype(jnp.float32) * pair_ok[:, None]
    rows_all = rows_per * tile_count
    grid_y = (
        (tile_pos * rows_per + jnp.arange(rows_per, dtype=jnp.int32)).astype(jnp.float32) + 0.5
    ) / rows_all * 2.0 - 1.0
    weight_y = weights * grid_y[None]
    partial = jnp.concatenate(
        [
            jnp.sum(weights, axis=1)[:, None],
            jnp.sum(weight_y, axis=1)[:, None],
            jnp.sum(weight_y * grid_y[None], axis=1)[:, None],
            jnp.sum(flow_est * weights[None], axis=2).T,
            jnp.sum(flow_est * weight_y[None], axis=2).T,
        ],
        axis=1,
    )
    totals = tile_sum(partial, "tile")
    weight_sum, weighted_y, weighted_yy = totals[:, 0], totals[:, 1], totals[:, 2]
    flow_sum = totals[:, 3:5].T
    flow_y_sum = totals[:, 5:7].T
    m_zero = weight_sum + RIDGE_TERM
    m_two = weighted_yy + RIDGE_TERM
    determinant = m_zero * m_two - weighted_y * weighted_y
    offset_coef = (m_two[None] * flow_sum - weighted_y[None] * flow_y_sum) / determinant[None]
    slope_coef = (m_zero[None] * flow_y_sum - weighted_y[None] * flow_sum) / determinant[None]
    affine = jnp.stack([offset_coef[0], slope_coef[0], offset_coef[1], slope_coef[1]], axis=1)
    fitted = offset_coef[:, :, None] + slope_coef[:, :, None] * grid_y[None, None, :]
    residual = (flow_est - fitted) * weights[None]
    return (residual, affine)


def solution(mesh):
    placed = (P("sec", "tile", None), P("sec"), P("sec", "tile"), P(), P(), P())
    return jax.shard_map(
        local,
        mesh=mesh,
        in_specs=placed,
        out_specs=(P(None, "sec", "tile"), P("sec", None)),
        check_vma=False,
    )
```
